32 devices in a mesh: ep: 8 (over z, x), tp: 4 (over y, core).
Axes of the slice: x: 2, y: 2, z: 4, core: 2. Of those that a mesh axis runs over, the one named last changes fastest.
Arguments:
- features: bfloat16 [2048, 1024], P('ep'), may hold values from -6 to 6
- cotangent: bfloat16 [2048, 2048], P('ep'), may hold values from -6 to 6
- expert_ids: int32 [2048, 2], P('ep'), may hold values from 0 to 7, all different within a row; in each aligned block of 256 rows (0 to 255, 256 to 511, ...) at most 96 rows name the same one
- gate_levels: int32 [2048, 2], P('ep'), may hold values from 1 to 15
- w_in: bfloat16 [8, 1024, 4096], P('ep', None, 'tp'), may hold values from -0.1875 to 0.1875
- w_out: bfloat16 [8, 4096, 2048], P('ep', 'tp'), may hold values from -0.09375 to 0.09375
Outputs:
- grad_in: bfloat16 [2048, 1024], P('ep', 'tp')
- grad_w_in: bfloat16 [8, 1024, 4096], P('ep', None, 'tp')
- grad_w_out: bfloat16 [8, 4096, 2048], P('ep', 'tp')
The draws below stay inside these ranges and needn't reach their ends.
Inputs may be any that keep to these rules, and one draw needn't show every extreme that they name: `expert_ids`: each row names two different experts. In each aligned block of 256 rows no expert is named by more than 96 rows, and some expert reaches 96 rows in some block.
All inputs are finite; a program needn't handle non-finite values.
Results may differ from the reference program's by a relative error of at most 0.0065.
Values may be sent and summed in bfloat16 or wider, within the bound.
No kernel may reach another device: no remote copies, remote signals or barrier semaphores. Data moves between devices by JAX's collectives and lax.ppermute only.
A program may use at most 128 MiB of HBM per device.

```python
import math
import jax
import jax.numpy as jnp
import numpy as np
from jax import lax

DIN = 1024
H = 4096
DOUT = 2048
E = 8
R = 1
SUB = 256
CAP = 96
TOKENS = 2048
N_EP = 8


def with_ends(drawn, stream_key, smallest, largest):
    dims = drawn.shape
    place = [jax.random.randint(jax.random.fold_in(stream_key, axis), (), 0, dims[axis]) for axis in range(len(dims))]
    drawn = drawn.at[tuple(place)].set(smallest)
    longest = dims.index(max(dims))
    place[longest] = (place[longest] + 1) % dims[longest]
    return drawn.at[tuple(place)].set(largest)


def block_levels(own_key, shape, split, smallest, high):
    level, own = 1.0, jax.random.fold_in(own_key, 6)
    for axis_at, blocks in split:
        heights = jnp.exp(jax.random.uniform(jax.random.fold_in(own, axis_at), (blocks,), jnp.float32, smallest / len(split), high / len(split)))
        level = level * jnp.repeat(heights, shape[axis_at] // blocks).reshape([-1 if axis == axis_at else 1 for axis in range(len(shape))])
    return level


def assign_block(own_key, own, number, rows, count, top, reach, lean):
    sequence = jax.random.permutation(own_key, count)
    heavy_load, usual = shares(count, rows * top, reach, lean, True), shares(count, rows * top, reach, lean, False)
    places = jnp.arange(count)

    def named(sizes, rotation):
        used = int((sizes > 0).sum())
        fixed = max(1, used // 4)
        passed = fixed + (places - fixed + rotation * (used - fixed)) % max(1, count - fixed)
        return jnp.zeros((count,), jnp.int32).at[sequence[jnp.where(places < fixed, places, passed)]].set(jnp.asarray(sizes, jnp.int32))

    sizes = jnp.where(number % 4 == 0, named(heavy_load, number // 4), named(usual, number - number // 4 - 1))
    mixed = jax.random.permutation(jax.random.fold_in(own, 3), count)
    donor, receiver = mixed[0:count // 2 * 2:2], mixed[1:count // 2 * 2:2]
    room = jnp.minimum(sizes[donor] - 1, reach - sizes[receiver]) // 2
    room = jnp.where((donor == sequence[0]) | (receiver == sequence[0]) | (sizes[receiver] == 0), 0, jnp.maximum(room, 0))
    passed = jax.random.randint(jax.random.fold_in(own, 4), (count // 2,), 0, 1 << 20) % (room + 1)
    sizes = sizes.at[donor].add(-passed).at[receiver].add(passed)
    items = jnp.searchsorted(jnp.cumsum(sizes), jnp.arange(rows * top), side="right").astype(jnp.int32)
    listing = items.reshape(top, rows).T
    listing = listing[jax.random.permutation(jax.random.fold_in(own, 1), rows)]
    rotation = jax.random.randint(jax.random.fold_in(own, 2), (rows, 1), 0, top)
    return jnp.take_along_axis(listing, (jnp.arange(top)[None, :] + rotation) % top, axis=1)


def shares(number_of, total, limit, slope, full):
    loads = [(1 << 20) // math.isqrt(rank ** slope) + 1 for rank in range(1, number_of + 1)]
    largest = limit if full else min(limit, max(-(-total // number_of), total * loads[0] // sum(loads)))
    least = 1 if total - largest >= number_of - 1 else 0
    counts, rest = [largest] + [least] * (number_of - 1), total - largest - least * (number_of - 1)
    while rest > 0:
        candidates = [i for i in range(1, number_of) if counts[i] < largest] or [i for i in range(1, number_of) if counts[i] < limit]
        whole, left = sum([loads[i] for i in candidates]), rest
        for i in candidates:
            addition = min(limit - counts[i], max(1, left * loads[i] // whole), rest)
            counts[i] = counts[i] + addition
            rest = rest - addition
    return np.array(counts)


def noise(key, extent, scale, limit, pieces=(), kind=jnp.bfloat16):
    entries = scale * jax.random.normal(key, extent, jnp.float32)
    if pieces:
        entries = entries * block_levels(key, extent, pieces, -0.22, 0.18)
    return jnp.clip(entries, -limit, limit).astype(kind)


def setup_inputs(seed: int = 0) -> dict:
    seeds = jax.random.split(jax.random.key(seed), 7)
    features = noise(seeds[0], (TOKENS, DIN), 1.0, 6.0, ((0, 8),))
    cotangent = noise(seeds[1], (TOKENS, DOUT), 1.0, 6.0, ((0, 8),))
    expert_ids_keys = jax.random.split(jax.random.fold_in(seeds[2], 1), TOKENS // SUB)
    expert_ids_turns = jax.random.permutation(jax.random.fold_in(seeds[2], 3), TOKENS // SUB)
    expert_ids = jax.vmap(lambda own, number: assign_block(jax.random.fold_in(seeds[2], 2), own, number, SUB, E, 2, CAP, 2))(expert_ids_keys, expert_ids_turns).reshape((TOKENS, 2))
    gate_levels = with_ends(jax.random.randint(seeds[3], (TOKENS, 2), 1, 16), jax.random.fold_in(seeds[3], 1), 1, 15).astype(jnp.int32)
    w_in = noise(seeds[4], (N_EP, DIN, H // R), DIN ** -0.5, 0.1875, ((0, 8), (2, 4)))
    w_out = noise(seeds[5], (N_EP, H // R, DOUT), H ** -0.5, 0.09375, ((0, 8), (1, 4)))
    return dict(features=features, cotangent=cotangent, expert_ids=expert_ids, gate_levels=gate_levels, w_in=w_in, w_out=w_out)


def reference(features, cotangent, expert_ids, gate_levels, w_in, w_out):
    block_count = TOKENS // SUB
    flattened = expert_ids.reshape(block_count, 2 * SUB)
    one_hot = (flattened[:, :, None] == jnp.arange(E, dtype=jnp.int32)[None, None, :]).astype(jnp.int32)
    earlier = jnp.cumsum(one_hot, axis=1) - one_hot
    within = lax.optimization_barrier(jnp.sum(one_hot * earlier, axis=2)).astype(jnp.int32)
    block_ids = jnp.arange(block_count, dtype=jnp.int32)[:, None]
    buffer_rows = block_count * CAP
    pair_count = 2 * TOKENS
    pair_range = jnp.arange(pair_count, dtype=jnp.int32)
    gate_values = gate_levels.reshape(-1).astype(jnp.float32) / 16.0
    grad_scale = 1.0 / math.sqrt(2.0 * TOKENS / E)
    hidden_part = H // R
    input_total = jnp.zeros((TOKENS, DIN), jnp.float32)
    grads_first = []
    grads_second = []
    for expert in range(E):
        target = jnp.where(flattened == expert, block_ids * CAP + within, buffer_rows).reshape(-1).astype(jnp.int32)
        owner = jnp.full((buffer_rows,), pair_count, jnp.int32).at[target].set(pair_range, mode='drop')
        filled = owner < pair_count
        pair_ids = jnp.minimum(owner, pair_count - 1).astype(jnp.int32)
        token_ids = (pair_ids // 2).astype(jnp.int32)
        rows_x = features[token_ids] * filled.astype(jnp.bfloat16)[:, None]
        slot_gates = jnp.where(filled, gate_values[pair_ids], jnp.float32(0.0))
        rows_dy = (cotangent[token_ids].astype(jnp.float32) * slot_gates[:, None]).astype(jnp.bfloat16)
        weight_in = jnp.concatenate([w_in[replica * E + expert] for replica in range(R)], axis=1)
        weight_out = jnp.concatenate([w_out[replica * E + expert] for replica in range(R)], axis=0)
        pre = jnp.dot(rows_x, weight_in, preferred_element_type=jnp.float32)
        activated, gelu_back = jax.vjp(jax.nn.gelu, pre)
        act_rows = activated.astype(jnp.bfloat16)
        back_act = jnp.dot(rows_dy, weight_out.T, preferred_element_type=jnp.float32)
        back_pre = gelu_back(back_act)[0].astype(jnp.bfloat16)
        second = jnp.dot(act_rows.T, rows_dy, preferred_element_type=jnp.float32)
        grads_second.append((second * grad_scale).astype(jnp.bfloat16))
        first = jnp.dot(rows_x.T, back_pre, preferred_element_type=jnp.float32)
        grads_first.append((first * grad_scale).astype(jnp.bfloat16))
        slot_input = jnp.dot(back_pre, weight_in.T, preferred_element_type=jnp.float32).astype(jnp.bfloat16)
        input_total = input_total.at[token_ids].add(slot_input.astype(jnp.float32) * filled.astype(jnp.float32)[:, None])
    grad_in = input_total.astype(jnp.bfloat16)
    grad_w_in = jnp.stack([grads_first[device % E][:, device // E * hidden_part:(device // E + 1) * hidden_part] for device in range(N_EP)])
    grad_w_out = jnp.stack([grads_second[device % E][device // E * hidden_part:(device // E + 1) * hidden_part, :] for device in range(N_EP)])
    return (grad_in, grad_w_in, grad_w_out)
```

```python
import math

import jax
import jax.numpy as jnp
from jax import lax
from jax.sharding import PartitionSpec as P

E = 8


def shifted(value, axis, by):
    peers = lax.axis_size(axis)
    return lax.ppermute(value, axis, [(i, (i + by) % peers) for i in range(peers)])


def slot_positions(expert_ids, blocks, experts, capacity):
    flattened = expert_ids.reshape(blocks, -1)
    one_hot = (flattened[:, :, None] == jnp.arange(experts, dtype=jnp.int32)[None, None, :]).astype(
        jnp.int32
    )
    earlier = jnp.cumsum(one_hot, axis=1) - one_hot
    within = jnp.sum(one_hot * earlier, axis=2)
    block_ids = jnp.arange(blocks, dtype=jnp.int32)[:, None]
    return ((block_ids * experts + flattened) * capacity + within).reshape(-1)


def chip_then_link_sum(partial, j):
    quarter = partial.shape[0] // 4

    def rows(q):
        return lax.dynamic_slice_in_dim(partial, q * quarter, quarter, 0)

    keep = jnp.concatenate([rows(j), rows(j ^ 2)], axis=0)
    give = jnp.concatenate([rows(j ^ 1), rows(j ^ 3)], axis=0)
    keep = keep + lax.ppermute(give, "tp", [(i, i ^ 1) for i in range(4)])
    mine, send = keep[:quarter], keep[quarter:]
    return mine + lax.ppermute(send, "tp", [(i, i ^ 2) for i in range(4)])


def shards(features, cotangent, expert_ids, gate_levels, w_in, w_out):
    device_count = lax.axis_size("ep")
    replicas = device_count // E
    replica = lax.axis_index("ep") // E
    tokens_here = expert_ids.shape[0]
    sub_rows = tokens_here // replicas
    capacity = 3 * sub_rows // 8
    slot_count = device_count * capacity
    pair_count = 2 * tokens_here
    positions = slot_positions(expert_ids, replicas, E, capacity)
    owner = (
        jnp.full((slot_count,), pair_count, jnp.int32)
        .at[positions]
        .set(jnp.arange(pair_count, dtype=jnp.int32))
    )
    filled = owner < pair_count
    pair_ids = jnp.minimum(owner, pair_count - 1)
    token_ids = pair_ids // 2
    gate_values = gate_levels.reshape(-1).astype(jnp.float32) / 16.0
    slot_gates = jnp.where(filled, gate_values[pair_ids], 0.0)
    slot_mask = filled.astype(jnp.bfloat16)[:, None]
    tp_size = lax.axis_size("tp")
    tp_index = lax.axis_index("tp")
    split = 2 if tp_size % 2 == 0 else 1
    half = tp_index % split

    def dispatched(table, scale):
        width = table.shape[1] // split
        mine = lax.dynamic_slice_in_dim(table, half * width, width, 1)[token_ids]
        mine = (mine.astype(jnp.float32) * scale).astype(jnp.bfloat16)
        mine = lax.all_to_all(mine, "ep", split_axis=0, concat_axis=0, tiled=True)
        if split == 1:
            return mine
        other = lax.ppermute(mine, "tp", [(i, i ^ 1) for i in range(tp_size)])
        whole = jnp.zeros((mine.shape[0], table.shape[1]), jnp.bfloat16)
        whole = lax.dynamic_update_slice_in_dim(whole, mine, half * width, 1)
        return lax.dynamic_update_slice_in_dim(whole, other, (1 - half) * width, 1)

    rows_x = dispatched(features, slot_mask.astype(jnp.float32))
    rows_dy = dispatched(cotangent, slot_gates[:, None])
    piece_in = w_in[0]
    piece_out = w_out[0]
    span = piece_in.shape[1]
    weight_in = jnp.zeros((piece_in.shape[0], span * replicas), jnp.bfloat16)
    weight_out = jnp.zeros((span * replicas, piece_out.shape[1]), jnp.bfloat16)
    weight_in = lax.dynamic_update_slice_in_dim(weight_in, piece_in, replica * span, 1)
    weight_out = lax.dynamic_update_slice_in_dim(weight_out, piece_out, replica * span, 0)
    moving = (piece_in, piece_out)
    for turn_index in range(1, replicas):
        moving = shifted((moving[0], moving[1]), "ep", E)
        anchor = (replica - turn_index) % replicas
        weight_in = lax.dynamic_update_slice_in_dim(weight_in, moving[0], anchor * span, 1)
        weight_out = lax.dynamic_update_slice_in_dim(weight_out, moving[1], anchor * span, 0)
    pre = jnp.dot(rows_x, weight_in, preferred_element_type=jnp.float32)
    activated, gelu_back = jax.vjp(jax.nn.gelu, pre)
    act_rows = activated.astype(jnp.bfloat16)
    back_act = lax.dot_general(
        rows_dy, weight_out, (((1,), (1,)), ((), ())), preferred_element_type=jnp.float32
    )
    back_pre = gelu_back(back_act)[0].astype(jnp.bfloat16)
    partial = lax.dot_general(
        weight_in, back_pre, (((1,), (1,)), ((), ())), preferred_element_type=jnp.float32
    )
    if tp_size == 4:
        summed = chip_then_link_sum(partial, tp_index)
    else:
        summed = lax.psum_scatter(partial, "tp", scatter_dimension=0, tiled=True)
    returned = lax.all_to_all(
        summed.astype(jnp.bfloat16), "ep", split_axis=1, concat_axis=1, tiled=True
    )
    picked = returned[:, positions].astype(jnp.float32)
    grad_in = jnp.sum(picked.reshape(picked.shape[0], tokens_here, 2), axis=2).T.astype(
        jnp.bfloat16
    )

    def span_grads(first_span, span_total):
        width = span_total * span
        act_cols = lax.dynamic_slice_in_dim(act_rows, first_span * span, width, 1)
        pre_cols = lax.dynamic_slice_in_dim(back_pre, first_span * span, width, 1)
        grad_first = lax.dot_general(
            pre_cols, rows_x, (((0,), (0,)), ((), ())), preferred_element_type=jnp.float32
        )
        grad_second = lax.dot_general(
            act_cols, rows_dy, (((0,), (0,)), ((), ())), preferred_element_type=jnp.float32
        )
        return (grad_first, grad_second)

    summed_grads = span_grads((replica - 1) % replicas, 1)
    for turn_index in range(1, replicas):
        summed_grads = shifted((summed_grads[0], summed_grads[1]), "ep", E)
        own_grads = span_grads((replica - turn_index - 1) % replicas, 1)
        summed_grads = (summed_grads[0] + own_grads[0], summed_grads[1] + own_grads[1])
    grad_scale = 1.0 / math.sqrt(2.0 * tokens_here * device_count / E)
    grad_w_in = (summed_grads[0] * grad_scale).T.astype(jnp.bfloat16)[None]
    grad_w_out = (summed_grads[1] * grad_scale).astype(jnp.bfloat16)[None]
    return (grad_in, grad_w_in, grad_w_out)


def solution(mesh):
    return jax.shard_map(
        shards,
        mesh=mesh,
        in_specs=(
            P("ep", None),
            P("ep", None),
            P("ep", None),
            P("ep", None),
            P("ep", None, "tp"),
            P("ep", "tp", None),
        ),
        out_specs=(P("ep", "tp"), P("ep", None, "tp"), P("ep", "tp", None)),
        check_vma=False,
    )
```

```python
import math

import jax
import jax.numpy as jnp
from jax import lax
from jax.sharding import PartitionSpec as P

E = 8


def shifted(value, axis, by):
    peers = lax.axis_size(axis)
    return lax.ppermute(value, axis, [(i, (i + by) % peers) for i in range(peers)])


def slot_positions(expert_ids, blocks, experts, capacity):
    flattened = expert_ids.reshape(blocks, -1)
    one_hot = (flattened[:, :, None] == jnp.arange(experts, dtype=jnp.int32)[None, None, :]).astype(
        jnp.int32
    )
    earlier = jnp.cumsum(one_hot, axis=1) - one_hot
    within = jnp.sum(one_hot * earlier, axis=2)
    block_ids = jnp.arange(blocks, dtype=jnp.int32)[:, None]
    return ((block_ids * experts + flattened) * capacity + within).reshape(-1)


def chip_then_link_sum(partial, j):
    quarter = partial.shape[0] // 4

    def rows(q):
        return lax.dynamic_slice_in_dim(partial, q * quarter, quarter, 0)

    keep = jnp.concatenate([rows(j), rows(j ^ 2)], axis=0)
    give = jnp.concatenate([rows(j ^ 1), rows(j ^ 3)], axis=0)
    keep = keep + lax.ppermute(give, "tp", [(i, i ^ 1) for i in range(4)])
    mine, send = keep[:quarter], keep[quarter:]
    return mine + lax.ppermute(send, "tp", [(i, i ^ 2) for i in range(4)])


def shards(features, cotangent, expert_ids, gate_levels, w_in, w_out):
    device_count = lax.axis_size("ep")
    replicas = device_count // E
    replica = lax.axis_index("ep") // E
    tokens_here = expert_ids.shape[0]
    sub_rows = tokens_here // replicas
    capacity = 3 * sub_rows // 8
    slot_count = device_count * capacity
    pair_count = 2 * tokens_here
    positions = slot_positions(expert_ids, replicas, E, capacity)
    slot_ids = jnp.arange(slot_count, dtype=jnp.int32)[:, None]
    choices = positions.reshape(tokens_here, 2)
    first_hit = choices[None, :, 0] == slot_ids
    second_hit = choices[None, :, 1] == slot_ids
    gates = gate_levels.astype(jnp.float32) / 16.0
    pick = (first_hit | second_hit).astype(jnp.bfloat16)
    pick_scaled = jnp.where(
        first_hit, gates[None, :, 0], jnp.where(second_hit, gates[None, :, 1], 0.0)
    ).astype(jnp.bfloat16)
    tp_size = lax.axis_size("tp")
    tp_index = lax.axis_index("tp")
    split = 2 if tp_size % 2 == 0 else 1
    half = tp_index % split

    def dispatched(table, selection):
        width = table.shape[1] // split
        mine = lax.dynamic_slice_in_dim(table, half * width, width, 1)
        mine = jnp.dot(selection, mine, preferred_element_type=jnp.float32).astype(jnp.bfloat16)
        mine = lax.all_to_all(mine, "ep", split_axis=0, concat_axis=0, tiled=True)
        if split == 1:
            return mine
        other = lax.ppermute(mine, "tp", [(i, i ^ 1) for i in range(tp_size)])
        whole = jnp.zeros((mine.shape[0], table.shape[1]), jnp.bfloat16)
        whole = lax.dynamic_update_slice_in_dim(whole, mine, half * width, 1)
        return lax.dynamic_update_slice_in_dim(whole, other, (1 - half) * width, 1)

    rows_x = dispatched(features, pick)
    rows_dy = dispatched(cotangent, pick_scaled)
    piece_in = w_in[0]
    piece_out = w_out[0]
    span = piece_in.shape[1]
    weight_in = jnp.zeros((piece_in.shape[0], span * replicas), jnp.bfloat16)
    weight_out = jnp.zeros((span * replicas, piece_out.shape[1]), jnp.bfloat16)
    weight_in = lax.dynamic_update_slice_in_dim(weight_in, piece_in, replica * span, 1)
    weight_out = lax.dynamic_update_slice_in_dim(weight_out, piece_out, replica * span, 0)
    moving = (piece_in, piece_out)
    for turn_index in range(1, replicas):
        moving = shifted((moving[0], moving[1]), "ep", E)
        anchor = (replica - turn_index) % replicas
        weight_in = lax.dynamic_update_slice_in_dim(weight_in, moving[0], anchor * span, 1)
        weight_out = lax.dynamic_update_slice_in_dim(weight_out, moving[1], anchor * span, 0)
    pre = jnp.dot(rows_x, weight_in, preferred_element_type=jnp.float32)
    activated, gelu_back = jax.vjp(jax.nn.gelu, pre)
    act_rows = activated.astype(jnp.bfloat16)
    back_act = lax.dot_general(
        rows_dy, weight_out, (((1,), (1,)), ((), ())), preferred_element_type=jnp.float32
    )
    back_pre = gelu_back(back_act)[0].astype(jnp.bfloat16)
    partial = lax.dot_general(
        weight_in, back_pre, (((1,), (1,)), ((), ())), preferred_element_type=jnp.float32
    )
    if tp_size == 4:
        summed = chip_then_link_sum(partial, tp_index)
    else:
        summed = lax.psum_scatter(partial, "tp", scatter_dimension=0, tiled=True)
    returned = lax.all_to_all(
        summed.astype(jnp.bfloat16), "ep", split_axis=1, concat_axis=1, tiled=True
    )
    grad_in = lax.dot_general(
        pick, returned, (((0,), (1,)), ((), ())), preferred_element_type=jnp.float32
    ).astype(jnp.bfloat16)

    def span_grads(first_span, span_total):
        width = span_total * span
        act_cols = lax.dynamic_slice_in_dim(act_rows, first_span * span, width, 1)
        pre_cols = lax.dynamic_slice_in_dim(back_pre, first_span * span, width, 1)
        grad_first = lax.dot_general(
            pre_cols, rows_x, (((0,), (0,)), ((), ())), preferred_element_type=jnp.float32
        )
        grad_second = lax.dot_general(
            act_cols, rows_dy, (((0,), (0,)), ((), ())), preferred_element_type=jnp.float32
        )
        return (grad_first, grad_second)

    summed_grads = span_grads((replica - 1) % replicas, 1)
    for turn_index in range(1, replicas):
        summed_grads = shifted((summed_grads[0], summed_grads[1]), "ep", E)
        own_grads = span_grads((replica - turn_index - 1) % replicas, 1)
        summed_grads = (summed_grads[0] + own_grads[0], summed_grads[1] + own_grads[1])
    grad_scale = 1.0 / math.sqrt(2.0 * tokens_here * device_count / E)
    grad_w_in = (summed_grads[0] * grad_scale).T.astype(jnp.bfloat16)[None]
    grad_w_out = (summed_grads[1] * grad_scale).astype(jnp.bfloat16)[None]
    return (grad_in, grad_w_in, grad_w_out)


def solution(mesh):
    return jax.shard_map(
        shards,
        mesh=mesh,
        in_specs=(
            P("ep", None),
            P("ep", None),
            P("ep", None),
            P("ep", None),
            P("ep", None, "tp"),
            P("ep", "tp", None),
        ),
        out_specs=(P("ep", "tp"), P("ep", None, "tp"), P("ep", "tp", None)),
        check_vma=False,
    )
```

```python
import math

import jax
import jax.numpy as jnp
from jax import lax
from jax.sharding import PartitionSpec as P

E = 8


def shifted(value, axis, by):
    peers = lax.axis_size(axis)
    return lax.ppermute(value, axis, [(i, (i + by) % peers) for i in range(peers)])


def slot_positions(expert_ids, blocks, experts, capacity):
    flattened = expert_ids.reshape(blocks, -1)
    one_hot = (flattened[:, :, None] == jnp.arange(experts, dtype=jnp.int32)[None, None, :]).astype(
        jnp.int32
    )
    earlier = jnp.cumsum(one_hot, axis=1) - one_hot
    within = jnp.sum(one_hot * earlier, axis=2)
    block_ids = jnp.arange(blocks, dtype=jnp.int32)[:, None]
    return ((block_ids * experts + flattened) * capacity + within).reshape(-1)


def chip_then_link_sum(partial, j):
    quarter = partial.shape[0] // 4

    def rows(q):
        return lax.dynamic_slice_in_dim(partial, q * quarter, quarter, 0)

    keep = jnp.concatenate([rows(j), rows(j ^ 2)], axis=0)
    give = jnp.concatenate([rows(j ^ 1), rows(j ^ 3)], axis=0)
    keep = keep + lax.ppermute(give, "tp", [(i, i ^ 1) for i in range(4)])
    mine, send = keep[:quarter], keep[quarter:]
    return mine + lax.ppermute(send, "tp", [(i, i ^ 2) for i in range(4)])


def shards(features, cotangent, expert_ids, gate_levels, w_in, w_out):
    device_count = lax.axis_size("ep")
    replicas = device_count // E
    replica = lax.axis_index("ep") // E
    tokens_here = expert_ids.shape[0]
    sub_rows = tokens_here // replicas
    capacity = 3 * sub_rows // 8
    slot_count = device_count * capacity
    pair_count = 2 * tokens_here
    positions = slot_positions(expert_ids, replicas, E, capacity)
    slot_ids = jnp.arange(slot_count, dtype=jnp.int32)[:, None]
    choices = positions.reshape(tokens_here, 2)
    first_hit = choices[None, :, 0] == slot_ids
    second_hit = choices[None, :, 1] == slot_ids
    gates = gate_levels.astype(jnp.float32) / 16.0
    pick = (first_hit | second_hit).astype(jnp.bfloat16)
    pick_scaled = jnp.where(
        first_hit, gates[None, :, 0], jnp.where(second_hit, gates[None, :, 1], 0.0)
    ).astype(jnp.bfloat16)
    tp_size = lax.axis_size("tp")
    tp_index = lax.axis_index("tp")
    split = 4 if tp_size == 4 else (2 if tp_size % 2 == 0 else 1)

    def dispatched(table, selection):
        width = table.shape[1] // split
        part = tp_index % split
        mine = lax.dynamic_slice_in_dim(table, part * width, width, 1)
        mine = jnp.dot(selection, mine, preferred_element_type=jnp.float32).astype(jnp.bfloat16)
        mine = lax.all_to_all(mine, "ep", split_axis=0, concat_axis=0, tiled=True)
        pieces = [(mine, part)]
        if split == 4:
            across = lax.ppermute(mine, "tp", [(i, i ^ 2) for i in range(tp_size)])
            pieces.append((across, part ^ 2))
        if split >= 2:
            pieces += [
                (lax.ppermute(piece, "tp", [(i, i ^ 1) for i in range(tp_size)]), where ^ 1)
                for piece, where in pieces
            ]
        if split == 1:
            return mine
        whole = jnp.zeros((mine.shape[0], table.shape[1]), jnp.bfloat16)
        for piece, where in pieces:
            whole = lax.dynamic_update_slice_in_dim(whole, piece, where * width, 1)
        return whole

    rows_x = dispatched(features, pick)
    rows_dy = dispatched(cotangent, pick_scaled)
    piece_in = w_in[0]
    piece_out = w_out[0]
    span = piece_in.shape[1]
    weight_in = jnp.zeros((piece_in.shape[0], span * replicas), jnp.bfloat16)
    weight_out = jnp.zeros((span * replicas, piece_out.shape[1]), jnp.bfloat16)
    weight_in = lax.dynamic_update_slice_in_dim(weight_in, piece_in, replica * span, 1)
    weight_out = lax.dynamic_update_slice_in_dim(weight_out, piece_out, replica * span, 0)
    moving = (piece_in, piece_out)
    for turn_index in range(1, replicas):
        moving = shifted((moving[0], moving[1]), "ep", E)
        anchor = (replica - turn_index) % replicas
        weight_in = lax.dynamic_update_slice_in_dim(weight_in, moving[0], anchor * span, 1)
        weight_out = lax.dynamic_update_slice_in_dim(weight_out, moving[1], anchor * span, 0)
    pre = jnp.dot(rows_x, weight_in, preferred_element_type=jnp.float32)
    activated, gelu_back = jax.vjp(jax.nn.gelu, pre)
    act_rows = activated.astype(jnp.bfloat16)
    back_act = lax.dot_general(
        rows_dy, weight_out, (((1,), (1,)), ((), ())), preferred_element_type=jnp.float32
    )
    back_pre = gelu_back(back_act)[0].astype(jnp.bfloat16)
    partial = lax.dot_general(
        weight_in, back_pre, (((1,), (1,)), ((), ())), preferred_element_type=jnp.float32
    )
    if tp_size == 4:
        summed = chip_then_link_sum(partial, tp_index)
    else:
        summed = lax.psum_scatter(partial, "tp", scatter_dimension=0, tiled=True)
    returned = lax.all_to_all(
        summed.astype(jnp.bfloat16), "ep", split_axis=1, concat_axis=1, tiled=True
    )
    grad_in = lax.dot_general(
        pick, returned, (((0,), (1,)), ((), ())), preferred_element_type=jnp.float32
    ).astype(jnp.bfloat16)

    def span_grads(first_span, span_total):
        width = span_total * span
        act_cols = lax.dynamic_slice_in_dim(act_rows, first_span * span, width, 1)
        pre_cols = lax.dynamic_slice_in_dim(back_pre, first_span * span, width, 1)
        grad_first = lax.dot_general(
            pre_cols, rows_x, (((0,), (0,)), ((), ())), preferred_element_type=jnp.float32
        )
        grad_second = lax.dot_general(
            act_cols, rows_dy, (((0,), (0,)), ((), ())), preferred_element_type=jnp.float32
        )
        return (grad_first, grad_second)

    summed_grads = span_grads((replica - 1) % replicas, 1)
    for turn_index in range(1, replicas):
        summed_grads = shifted((summed_grads[0], summed_grads[1]), "ep", E)
        own_grads = span_grads((replica - turn_index - 1) % replicas, 1)
        summed_grads = (summed_grads[0] + own_grads[0], summed_grads[1] + own_grads[1])
    grad_scale = 1.0 / math.sqrt(2.0 * tokens_here * device_count / E)
    grad_w_in = (summed_grads[0] * grad_scale).T.astype(jnp.bfloat16)[None]
    grad_w_out = (summed_grads[1] * grad_scale).astype(jnp.bfloat16)[None]
    return (grad_in, grad_w_in, grad_w_out)


def solution(mesh):
    return jax.shard_map(
        shards,
        mesh=mesh,
        in_specs=(
            P("ep", None),
            P("ep", None),
            P("ep", None),
            P("ep", None),
            P("ep", None, "tp"),
            P("ep", "tp", None),
        ),
        out_specs=(P("ep", "tp"), P("ep", None, "tp"), P("ep", "tp", None)),
        check_vma=False,
    )
```

```python
import math

import jax
import jax.numpy as jnp
from jax import lax
from jax.sharding import PartitionSpec as P

E = 8


def shifted(value, axis, by):
    peers = lax.axis_size(axis)
    return lax.ppermute(value, axis, [(i, (i + by) % peers) for i in range(peers)])


def slot_positions(expert_ids, blocks, experts, capacity):
    flattened = expert_ids.reshape(blocks, -1)
    one_hot = (flattened[:, :, None] == jnp.arange(experts, dtype=jnp.int32)[None, None, :]).astype(
        jnp.int32
    )
    earlier = jnp.cumsum(one_hot, axis=1) - one_hot
    within = jnp.sum(one_hot * earlier, axis=2)
    block_ids = jnp.arange(blocks, dtype=jnp.int32)[:, None]
    return ((block_ids * experts + flattened) * capacity + within).reshape(-1)


def chip_then_link_sum(partial, j):
    quarter = partial.shape[0] // 4

    def rows(q):
        return lax.dynamic_slice_in_dim(partial, q * quarter, quarter, 0)

    keep = jnp.concatenate([rows(j), rows(j ^ 2)], axis=0)
    give = jnp.concatenate([rows(j ^ 1), rows(j ^ 3)], axis=0)
    keep = keep + lax.ppermute(give, "tp", [(i, i ^ 1) for i in range(4)])
    mine, send = keep[:quarter], keep[quarter:]
    moved = lax.ppermute(send.astype(jnp.bfloat16), "tp", [(i, i ^ 2) for i in range(4)])
    return mine + moved.astype(jnp.float32)


def shards(features, cotangent, expert_ids, gate_levels, w_in, w_out):
    device_count = lax.axis_size("ep")
    replicas = device_count // E
    replica = lax.axis_index("ep") // E
    tokens_here = expert_ids.shape[0]
    sub_rows = tokens_here // replicas
    capacity = 3 * sub_rows // 8
    slot_count = device_count * capacity
    pair_count = 2 * tokens_here
    positions = slot_positions(expert_ids, replicas, E, capacity)
    slot_ids = jnp.arange(slot_count, dtype=jnp.int32)[:, None]
    choices = positions.reshape(tokens_here, 2)
    first_hit = choices[None, :, 0] == slot_ids
    second_hit = choices[None, :, 1] == slot_ids
    gates = gate_levels.astype(jnp.float32) / 16.0
    pick = (first_hit | second_hit).astype(jnp.bfloat16)
    pick_scaled = jnp.where(
        first_hit, gates[None, :, 0], jnp.where(second_hit, gates[None, :, 1], 0.0)
    ).astype(jnp.bfloat16)
    tp_size = lax.axis_size("tp")
    tp_index = lax.axis_index("tp")
    split = 4 if tp_size == 4 else (2 if tp_size % 2 == 0 else 1)

    def dispatched(table, selection):
        width = table.shape[1] // split
        part = tp_index % split
        mine = lax.dynamic_slice_in_dim(table, part * width, width, 1)
        mine = jnp.dot(selection, mine, preferred_element_type=jnp.float32).astype(jnp.bfloat16)
        mine = lax.all_to_all(mine, "ep", split_axis=0, concat_axis=0, tiled=True)
        pieces = [(mine, part)]
        if split == 4:
            across = lax.ppermute(mine, "tp", [(i, i ^ 2) for i in range(tp_size)])
            pieces.append((across, part ^ 2))
        if split >= 2:
            pieces += [
                (lax.ppermute(piece, "tp", [(i, i ^ 1) for i in range(tp_size)]), where ^ 1)
                for piece, where in pieces
            ]
        if split == 1:
            return mine
        whole = jnp.zeros((mine.shape[0], table.shape[1]), jnp.bfloat16)
        for piece, where in pieces:
            whole = lax.dynamic_update_slice_in_dim(whole, piece, where * width, 1)
        return whole

    rows_x = dispatched(features, pick)
    rows_dy = dispatched(cotangent, pick_scaled)
    piece_in = w_in[0]
    piece_out = w_out[0]
    span = piece_in.shape[1]
    weight_in = jnp.zeros((piece_in.shape[0], span * replicas), jnp.bfloat16)
    weight_out = jnp.zeros((span * replicas, piece_out.shape[1]), jnp.bfloat16)
    weight_in = lax.dynamic_update_slice_in_dim(weight_in, piece_in, replica * span, 1)
    weight_out = lax.dynamic_update_slice_in_dim(weight_out, piece_out, replica * span, 0)
    moving = (piece_in, piece_out)
    for turn_index in range(1, replicas):
        moving = shifted((moving[0], moving[1]), "ep", E)
        anchor = (replica - turn_index) % replicas
        weight_in = lax.dynamic_update_slice_in_dim(weight_in, moving[0], anchor * span, 1)
        weight_out = lax.dynamic_update_slice_in_dim(weight_out, moving[1], anchor * span, 0)
    pre = jnp.dot(rows_x, weight_in, preferred_element_type=jnp.float32)
    activated, gelu_back = jax.vjp(jax.nn.gelu, pre)
    act_rows = lax.optimization_barrier(activated.astype(jnp.bfloat16))
    back_act = lax.dot_general(
        rows_dy, weight_out, (((1,), (1,)), ((), ())), preferred_element_type=jnp.float32
    )
    back_pre = gelu_back(back_act)[0].astype(jnp.bfloat16)
    partial = lax.dot_general(
        weight_in, back_pre, (((1,), (1,)), ((), ())), preferred_element_type=jnp.float32
    )
    if tp_size == 4:
        summed = chip_then_link_sum(partial, tp_index)
    else:
        summed = lax.psum_scatter(partial, "tp", scatter_dimension=0, tiled=True)
    returned = lax.all_to_all(
        summed.astype(jnp.bfloat16), "ep", split_axis=1, concat_axis=1, tiled=True
    )
    grad_in = lax.dot_general(
        pick, returned, (((0,), (1,)), ((), ())), preferred_element_type=jnp.float32
    ).astype(jnp.bfloat16)

    def span_grads(first_span, span_total):
        width = span_total * span
        act_cols = lax.dynamic_slice_in_dim(act_rows, first_span * span, width, 1)
        pre_cols = lax.dynamic_slice_in_dim(back_pre, first_span * span, width, 1)
        grad_first = lax.dot_general(
            pre_cols, rows_x, (((0,), (0,)), ((), ())), preferred_element_type=jnp.float32
        )
        grad_second = lax.dot_general(
            act_cols, rows_dy, (((0,), (0,)), ((), ())), preferred_element_type=jnp.float32
        )
        return (grad_first, grad_second)

    summed_grads = span_grads((replica - 1) % replicas, 1)
    for turn_index in range(1, replicas):
        summed_grads = shifted((summed_grads[0], summed_grads[1]), "ep", E)
        own_grads = span_grads((replica - turn_index - 1) % replicas, 1)
        summed_grads = (summed_grads[0] + own_grads[0], summed_grads[1] + own_grads[1])
    grad_scale = 1.0 / math.sqrt(2.0 * tokens_here * device_count / E)
    grad_w_in = (summed_grads[0] * grad_scale).T.astype(jnp.bfloat16)[None]
    grad_w_out = (summed_grads[1] * grad_scale).astype(jnp.bfloat16)[None]
    return (grad_in, grad_w_in, grad_w_out)


def solution(mesh):
    return jax.shard_map(
        shards,
        mesh=mesh,
        in_specs=(
            P("ep", None),
            P("ep", None),
            P("ep", None),
            P("ep", None),
            P("ep", None, "tp"),
            P("ep", "tp", None),
        ),
        out_specs=(P("ep", "tp"), P("ep", None, "tp"), P("ep", "tp", None)),
        check_vma=False,
    )
```

```python
import math

import jax
import jax.numpy as jnp
from jax import lax
from jax.sharding import PartitionSpec as P

E = 8


def shifted(value, axis, by):
    peers = lax.axis_size(axis)
    return lax.ppermute(value, axis, [(i, (i + by) % peers) for i in range(peers)])


def slot_positions(expert_ids, blocks, experts, capacity):
    flattened = expert_ids.reshape(blocks, -1)
    one_hot = (flattened[:, :, None] == jnp.arange(experts, dtype=jnp.int32)[None, None, :]).astype(
        jnp.int32
    )
    earlier = jnp.cumsum(one_hot, axis=1) - one_hot
    within = jnp.sum(one_hot * earlier, axis=2)
    block_ids = jnp.arange(blocks, dtype=jnp.int32)[:, None]
    return ((block_ids * experts + flattened) * capacity + within).reshape(-1)


def chip_then_link_sum(partial, j):
    quarter = partial.shape[0] // 4

    def rows(q):
        return lax.dynamic_slice_in_dim(partial, q * quarter, quarter, 0)

    keep = jnp.concatenate([rows(j), rows(j ^ 2)], axis=0)
    give = jnp.concatenate([rows(j ^ 1), rows(j ^ 3)], axis=0)
    keep = keep + lax.ppermute(give, "tp", [(i, i ^ 1) for i in range(4)])
    mine, send = keep[:quarter], keep[quarter:]
    return mine + lax.ppermute(send, "tp", [(i, i ^ 2) for i in range(4)])


def shards(features, cotangent, expert_ids, gate_levels, w_in, w_out):
    device_count = lax.axis_size("ep")
    replicas = device_count // E
    replica = lax.axis_index("ep") // E
    tokens_here = expert_ids.shape[0]
    sub_rows = tokens_here // replicas
    capacity = 3 * sub_rows // 8
    slot_count = device_count * capacity
    pair_count = 2 * tokens_here
    positions = slot_positions(expert_ids, replicas, E, capacity)
    slot_ids = jnp.arange(slot_count, dtype=jnp.int32)[:, None]
    choices = positions.reshape(tokens_here, 2)
    first_hit = choices[None, :, 0] == slot_ids
    second_hit = choices[None, :, 1] == slot_ids
    gates = gate_levels.astype(jnp.float32) / 16.0
    pick = (first_hit | second_hit).astype(jnp.bfloat16)
    pick_scaled = jnp.where(
        first_hit, gates[None, :, 0], jnp.where(second_hit, gates[None, :, 1], 0.0)
    ).astype(jnp.bfloat16)
    tp_size = lax.axis_size("tp")
    tp_index = lax.axis_index("tp")
    split = 4 if tp_size == 4 else (2 if tp_size % 2 == 0 else 1)

    chunks = 2 if capacity % 2 == 0 else 1

    def dispatched(tables, selections):
        part = tp_index % split
        widths = [table.shape[1] // split for table in tables]
        mine = jnp.concatenate(
            [
                jnp.dot(
                    selection,
                    lax.dynamic_slice_in_dim(table, part * width, width, 1),
                    preferred_element_type=jnp.float32,
                ).astype(jnp.bfloat16)
                for table, selection, width in zip(tables, selections, widths)
            ],
            axis=1,
        ).reshape(device_count, capacity, sum(widths))
        rows = capacity // chunks
        wholes = [
            jnp.zeros((device_count, capacity, table.shape[1]), jnp.bfloat16) for table in tables
        ]
        for chunk in range(chunks):
            block = mine[:, chunk * rows:(chunk + 1) * rows].reshape(device_count * rows, -1)
            block = lax.all_to_all(block, "ep", split_axis=0, concat_axis=0, tiled=True)
            pieces = [(block, part)]
            if split == 4:
                across = lax.ppermute(block, "tp", [(i, i ^ 2) for i in range(tp_size)])
                pieces.append((across, part ^ 2))
            if split >= 2:
                pieces += [
                    (lax.ppermute(piece, "tp", [(i, i ^ 1) for i in range(tp_size)]), where ^ 1)
                    for piece, where in pieces
                ]
            for piece, where in pieces:
                piece = piece.reshape(device_count, rows, -1)
                start = 0
                for index, width in enumerate(widths):
                    wholes[index] = lax.dynamic_update_slice(
                        wholes[index],
                        piece[:, :, start:start + width],
                        (0, chunk * rows, where * width),
                    )
                    start += width
        return [whole.reshape(slot_count, -1) for whole in wholes]

    rows_x, rows_dy = dispatched((features, cotangent), (pick, pick_scaled))
    piece_in = w_in[0]
    piece_out = w_out[0]
    span = piece_in.shape[1]
    weight_in = jnp.zeros((piece_in.shape[0], span * replicas), jnp.bfloat16)
    weight_out = jnp.zeros((span * replicas, piece_out.shape[1]), jnp.bfloat16)
    weight_in = lax.dynamic_update_slice_in_dim(weight_in, piece_in, replica * span, 1)
    weight_out = lax.dynamic_update_slice_in_dim(weight_out, piece_out, replica * span, 0)
    moving = (piece_in, piece_out)
    for turn_index in range(1, replicas):
        moving = shifted((moving[0], moving[1]), "ep", E)
        anchor = (replica - turn_index) % replicas
        weight_in = lax.dynamic_update_slice_in_dim(weight_in, moving[0], anchor * span, 1)
        weight_out = lax.dynamic_update_slice_in_dim(weight_out, moving[1], anchor * span, 0)
    pre = jnp.dot(rows_x, weight_in, preferred_element_type=jnp.float32)
    activated, gelu_back = jax.vjp(jax.nn.gelu, pre)
    act_rows = activated.astype(jnp.bfloat16)
    back_act = lax.dot_general(
        rows_dy, weight_out, (((1,), (1,)), ((), ())), preferred_element_type=jnp.float32
    )
    back_pre = gelu_back(back_act)[0].astype(jnp.bfloat16)
    partial = lax.dot_general(
        weight_in, back_pre, (((1,), (1,)), ((), ())), preferred_element_type=jnp.float32
    )
    if tp_size == 4:
        summed = chip_then_link_sum(partial, tp_index)
    else:
        summed = lax.psum_scatter(partial, "tp", scatter_dimension=0, tiled=True)
    returned = lax.all_to_all(
        summed.astype(jnp.bfloat16), "ep", split_axis=1, concat_axis=1, tiled=True
    )
    grad_in = lax.dot_general(
        pick, returned, (((0,), (1,)), ((), ())), preferred_element_type=jnp.float32
    ).astype(jnp.bfloat16)

    def span_grads(first_span, span_total):
        width = span_total * span
        act_cols = lax.dynamic_slice_in_dim(act_rows, first_span * span, width, 1)
        pre_cols = lax.dynamic_slice_in_dim(back_pre, first_span * span, width, 1)
        grad_first = lax.dot_general(
            pre_cols, rows_x, (((0,), (0,)), ((), ())), preferred_element_type=jnp.float32
        )
        grad_second = lax.dot_general(
            act_cols, rows_dy, (((0,), (0,)), ((), ())), preferred_element_type=jnp.float32
        )
        return (grad_first, grad_second)

    summed_grads = span_grads((replica - 1) % replicas, 1)
    for turn_index in range(1, replicas):
        summed_grads = shifted((summed_grads[0], summed_grads[1]), "ep", E)
        own_grads = span_grads((replica - turn_index - 1) % replicas, 1)
        summed_grads = (summed_grads[0] + own_grads[0], summed_grads[1] + own_grads[1])
    grad_scale = 1.0 / math.sqrt(2.0 * tokens_here * device_count / E)
    grad_w_in = (summed_grads[0] * grad_scale).T.astype(jnp.bfloat16)[None]
    grad_w_out = (summed_grads[1] * grad_scale).astype(jnp.bfloat16)[None]
    return (grad_in, grad_w_in, grad_w_out)


def solution(mesh):
    return jax.shard_map(
        shards,
        mesh=mesh,
        in_specs=(
            P("ep", None),
            P("ep", None),
            P("ep", None),
            P("ep", None),
            P("ep", None, "tp"),
            P("ep", "tp", None),
        ),
        out_specs=(P("ep", "tp"), P("ep", None, "tp"), P("ep", "tp", None)),
        check_vma=False,
    )
```

```python
import math

import jax
import jax.numpy as jnp
from jax import lax
from jax.sharding import PartitionSpec as P

E = 8


def shifted(value, axis, by):
    peers = lax.axis_size(axis)
    return lax.ppermute(value, axis, [(i, (i + by) % peers) for i in range(peers)])


def slot_positions(expert_ids, blocks, experts, capacity):
    flattened = expert_ids.reshape(blocks, -1)
    one_hot = (flattened[:, :, None] == jnp.arange(experts, dtype=jnp.int32)[None, None, :]).astype(
        jnp.int32
    )
    earlier = jnp.cumsum(one_hot, axis=1) - one_hot
    within = jnp.sum(one_hot * earlier, axis=2)
    block_ids = jnp.arange(blocks, dtype=jnp.int32)[:, None]
    return ((block_ids * experts + flattened) * capacity + within).reshape(-1)


def chip_then_link_sum(partial, j):
    quarter = partial.shape[0] // 4

    def rows(q):
        return lax.dynamic_slice_in_dim(partial, q * quarter, quarter, 0)

    keep = jnp.concatenate([rows(j), rows(j ^ 2)], axis=0)
    give = jnp.concatenate([rows(j ^ 1), rows(j ^ 3)], axis=0)
    keep = keep + lax.ppermute(give, "tp", [(i, i ^ 1) for i in range(4)])
    mine, send = keep[:quarter], keep[quarter:]
    return mine + lax.ppermute(send, "tp", [(i, i ^ 2) for i in range(4)])


def shards(features, cotangent, expert_ids, gate_levels, w_in, w_out):
    device_count = lax.axis_size("ep")
    replicas = device_count // E
    replica = lax.axis_index("ep") // E
    tokens_here = expert_ids.shape[0]
    sub_rows = tokens_here // replicas
    capacity = 3 * sub_rows // 8
    slot_count = device_count * capacity
    pair_count = 2 * tokens_here
    positions = slot_positions(expert_ids, replicas, E, capacity)
    slot_ids = jnp.arange(slot_count, dtype=jnp.int32)[:, None]
    choices = positions.reshape(tokens_here, 2)
    first_hit = choices[None, :, 0] == slot_ids
    second_hit = choices[None, :, 1] == slot_ids
    gates = gate_levels.astype(jnp.float32) / 16.0
    pick = (first_hit | second_hit).astype(jnp.bfloat16)
    pick_scaled = jnp.where(
        first_hit, gates[None, :, 0], jnp.where(second_hit, gates[None, :, 1], 0.0)
    ).astype(jnp.bfloat16)
    tp_size = lax.axis_size("tp")
    tp_index = lax.axis_index("tp")
    split = 4 if tp_size == 4 else (2 if tp_size % 2 == 0 else 1)

    def dispatched(table, selection):
        width = table.shape[1] // split
        part = tp_index % split
        mine = lax.dynamic_slice_in_dim(table, part * width, width, 1)
        mine = jnp.dot(selection, mine, preferred_element_type=jnp.float32).astype(jnp.bfloat16)
        mine = lax.all_to_all(mine, "ep", split_axis=0, concat_axis=0, tiled=True)
        pieces = [(mine, part)]
        if split == 4:
            across = lax.ppermute(mine, "tp", [(i, i ^ 2) for i in range(tp_size)])
            pieces.append((across, part ^ 2))
        if split >= 2:
            pieces += [
                (lax.ppermute(piece, "tp", [(i, i ^ 1) for i in range(tp_size)]), where ^ 1)
                for piece, where in pieces
            ]
        if split == 1:
            return mine
        whole = jnp.zeros((mine.shape[0], table.shape[1]), jnp.bfloat16)
        for piece, where in pieces:
            whole = lax.dynamic_update_slice_in_dim(whole, piece, where * width, 1)
        return whole

    rows_x = dispatched(features, pick)
    rows_dy = dispatched(cotangent, pick_scaled)
    piece_in = w_in[0]
    piece_out = w_out[0]
    span = piece_in.shape[1]
    weight_in = jnp.zeros((piece_in.shape[0], span * replicas), jnp.bfloat16)
    weight_out = jnp.zeros((span * replicas, piece_out.shape[1]), jnp.bfloat16)
    weight_in = lax.dynamic_update_slice_in_dim(weight_in, piece_in, replica * span, 1)
    weight_out = lax.dynamic_update_slice_in_dim(weight_out, piece_out, replica * span, 0)
    moving = (piece_in, piece_out)
    for turn_index in range(1, replicas):
        moving = shifted((moving[0], moving[1]), "ep", E)
        anchor = (replica - turn_index) % replicas
        weight_in = lax.dynamic_update_slice_in_dim(weight_in, moving[0], anchor * span, 1)
        weight_out = lax.dynamic_update_slice_in_dim(weight_out, moving[1], anchor * span, 0)
    pre = jnp.dot(rows_x, weight_in, preferred_element_type=jnp.float32)
    activated, gelu_back = jax.vjp(jax.nn.gelu, pre)
    act_rows = activated.astype(jnp.bfloat16)
    back_act = lax.dot_general(
        rows_dy, weight_out, (((1,), (1,)), ((), ())), preferred_element_type=jnp.float32
    )
    back_pre = gelu_back(back_act)[0].astype(jnp.bfloat16)
    partial = lax.dot_general(
        weight_in, back_pre, (((1,), (1,)), ((), ())), preferred_element_type=jnp.float32
    )
    if tp_size == 4:
        summed = chip_then_link_sum(partial, tp_index)
    else:
        summed = lax.psum_scatter(partial, "tp", scatter_dimension=0, tiled=True)
    def span_grads(first_span, span_total):
        width = span_total * span
        act_cols = lax.dynamic_slice_in_dim(act_rows, first_span * span, width, 1)
        pre_cols = lax.dynamic_slice_in_dim(back_pre, first_span * span, width, 1)
        grad_first = lax.dot_general(
            pre_cols, rows_x, (((0,), (0,)), ((), ())), preferred_element_type=jnp.float32
        )
        grad_second = lax.dot_general(
            act_cols, rows_dy, (((0,), (0,)), ((), ())), preferred_element_type=jnp.float32
        )
        return (grad_first, grad_second)

    summed_grads = span_grads((replica - 1) % replicas, 1)
    for turn_index in range(1, replicas):
        summed_grads = shifted((summed_grads[0], summed_grads[1]), "ep", E)
        own_grads = span_grads((replica - turn_index - 1) % replicas, 1)
        summed_grads = (summed_grads[0] + own_grads[0], summed_grads[1] + own_grads[1])
    grad_scale = 1.0 / math.sqrt(2.0 * tokens_here * device_count / E)
    grad_w_in = (summed_grads[0] * grad_scale).T.astype(jnp.bfloat16)[None]
    grad_w_out = (summed_grads[1] * grad_scale).astype(jnp.bfloat16)[None]
    leaving, grad_w_in, grad_w_out = lax.optimization_barrier(
        (summed.astype(jnp.bfloat16), grad_w_in, grad_w_out)
    )
    returned = lax.all_to_all(
        leaving, "ep", split_axis=1, concat_axis=1, tiled=True
    )
    grad_in = lax.dot_general(
        pick, returned, (((0,), (1,)), ((), ())), preferred_element_type=jnp.float32
    ).astype(jnp.bfloat16)
    return (grad_in, grad_w_in, grad_w_out)


def solution(mesh):
    return jax.shard_map(
        shards,
        mesh=mesh,
        in_specs=(
            P("ep", None),
            P("ep", None),
            P("ep", None),
            P("ep", None),
            P("ep", None, "tp"),
            P("ep", "tp", None),
        ),
        out_specs=(P("ep", "tp"), P("ep", None, "tp"), P("ep", "tp", None)),
        check_vma=False,
    )
```

```python
import math

import jax
import jax.numpy as jnp
from jax import lax
from jax.sharding import PartitionSpec as P

E = 8


def shifted(value, axis, by):
    peers = lax.axis_size(axis)
    return lax.ppermute(value, axis, [(i, (i + by) % peers) for i in range(peers)])


def slot_positions(expert_ids, blocks, experts, capacity):
    flattened = expert_ids.reshape(blocks, -1)
    one_hot = (flattened[:, :, None] == jnp.arange(experts, dtype=jnp.int32)[None, None, :]).astype(
        jnp.int32
    )
    earlier = jnp.cumsum(one_hot, axis=1) - one_hot
    within = jnp.sum(one_hot * earlier, axis=2)
    block_ids = jnp.arange(blocks, dtype=jnp.int32)[:, None]
    return ((block_ids * experts + flattened) * capacity + within).reshape(-1)


def chip_then_link_sum(partial, j):
    quarter = partial.shape[0] // 4

    def rows(q):
        return lax.dynamic_slice_in_dim(partial, q * quarter, quarter, 0)

    keep = jnp.concatenate([rows(j), rows(j ^ 2)], axis=0)
    give = jnp.concatenate([rows(j ^ 1), rows(j ^ 3)], axis=0)
    keep = keep + lax.ppermute(give, "tp", [(i, i ^ 1) for i in range(4)])
    mine, send = keep[:quarter], keep[quarter:]
    return mine + lax.ppermute(send, "tp", [(i, i ^ 2) for i in range(4)])


def shards(features, cotangent, expert_ids, gate_levels, w_in, w_out):
    device_count = lax.axis_size("ep")
    replicas = device_count // E
    replica = lax.axis_index("ep") // E
    tokens_here = expert_ids.shape[0]
    sub_rows = tokens_here // replicas
    capacity = 3 * sub_rows // 8
    slot_count = device_count * capacity
    pair_count = 2 * tokens_here
    positions = slot_positions(expert_ids, replicas, E, capacity)
    slot_ids = jnp.arange(slot_count, dtype=jnp.int32)[:, None]
    choices = positions.reshape(tokens_here, 2)
    first_hit = choices[None, :, 0] == slot_ids
    second_hit = choices[None, :, 1] == slot_ids
    gates = gate_levels.astype(jnp.float32) / 16.0
    pick = (first_hit | second_hit).astype(jnp.bfloat16)
    pick_scaled = jnp.where(
        first_hit, gates[None, :, 0], jnp.where(second_hit, gates[None, :, 1], 0.0)
    ).astype(jnp.bfloat16)
    tp_size = lax.axis_size("tp")
    tp_index = lax.axis_index("tp")
    split = 4 if tp_size == 4 else (2 if tp_size % 2 == 0 else 1)
    part = tp_index % split
    chunks = 2 if capacity % 2 == 0 else 1
    rows = capacity // chunks

    piece_in = w_in[0]
    piece_out = w_out[0]
    span = piece_in.shape[1]
    weight_in = jnp.zeros((piece_in.shape[0], span * replicas), jnp.bfloat16)
    weight_out = jnp.zeros((span * replicas, piece_out.shape[1]), jnp.bfloat16)
    weight_in = lax.dynamic_update_slice_in_dim(weight_in, piece_in, replica * span, 1)
    weight_out = lax.dynamic_update_slice_in_dim(weight_out, piece_out, replica * span, 0)
    moving = (piece_in, piece_out)
    for turn_index in range(1, replicas):
        moving = shifted((moving[0], moving[1]), "ep", E)
        anchor = (replica - turn_index) % replicas
        weight_in = lax.dynamic_update_slice_in_dim(weight_in, moving[0], anchor * span, 1)
        weight_out = lax.dynamic_update_slice_in_dim(weight_out, moving[1], anchor * span, 0)

    tables = (features, cotangent)
    widths = [table.shape[1] // split for table in tables]
    mine = jnp.concatenate(
        [
            jnp.dot(
                selection,
                lax.dynamic_slice_in_dim(table, part * width, width, 1),
                preferred_element_type=jnp.float32,
            ).astype(jnp.bfloat16)
            for table, selection, width in zip(tables, (pick, pick_scaled), widths)
        ],
        axis=1,
    ).reshape(device_count, capacity, sum(widths))

    def chunk_rows(chunk):
        block = mine[:, chunk * rows:(chunk + 1) * rows].reshape(device_count * rows, -1)
        block = lax.all_to_all(block, "ep", split_axis=0, concat_axis=0, tiled=True)
        pieces = [(block, part)]
        if split == 4:
            across = lax.ppermute(block, "tp", [(i, i ^ 2) for i in range(tp_size)])
            pieces.append((across, part ^ 2))
        if split >= 2:
            pieces += [
                (lax.ppermute(piece, "tp", [(i, i ^ 1) for i in range(tp_size)]), where ^ 1)
                for piece, where in pieces
            ]
        wholes = [
            jnp.zeros((device_count * rows, table.shape[1]), jnp.bfloat16) for table in tables
        ]
        for piece, where in pieces:
            start = 0
            for index, width in enumerate(widths):
                wholes[index] = lax.dynamic_update_slice_in_dim(
                    wholes[index], piece[:, start:start + width], where * width, 1
                )
                start += width
        return wholes

    def expert_rows(rows_x, rows_dy):
        pre = jnp.dot(rows_x, weight_in, preferred_element_type=jnp.float32)
        activated, gelu_back = jax.vjp(jax.nn.gelu, pre)
        act_rows = activated.astype(jnp.bfloat16)
        back_act = lax.dot_general(
            rows_dy, weight_out, (((1,), (1,)), ((), ())), preferred_element_type=jnp.float32
        )
        back_pre = gelu_back(back_act)[0].astype(jnp.bfloat16)
        partial = lax.dot_general(
            weight_in, back_pre, (((1,), (1,)), ((), ())), preferred_element_type=jnp.float32
        )
        if tp_size == 4:
            summed = chip_then_link_sum(partial, tp_index)
        else:
            summed = lax.psum_scatter(partial, "tp", scatter_dimension=0, tiled=True)
        grad_first = lax.dot_general(
            back_pre, rows_x, (((0,), (0,)), ((), ())), preferred_element_type=jnp.float32
        )
        grad_second = lax.dot_general(
            act_rows, rows_dy, (((0,), (0,)), ((), ())), preferred_element_type=jnp.float32
        )
        return summed, grad_first, grad_second

    selection = pick.reshape(device_count, capacity, tokens_here)
    grad_in = None
    totals = None
    for chunk in range(chunks):
        rows_x, rows_dy = chunk_rows(chunk)
        summed, grad_first, grad_second = expert_rows(rows_x, rows_dy)
        if totals is None:
            totals = (grad_first, grad_second)
        else:
            totals = (totals[0] + grad_first, totals[1] + grad_second)
        returned = lax.all_to_all(
            summed.astype(jnp.bfloat16), "ep", split_axis=1, concat_axis=1, tiled=True
        )
        chosen = selection[:, chunk * rows:(chunk + 1) * rows].reshape(device_count * rows, -1)
        term = lax.dot_general(
            chosen, returned, (((0,), (1,)), ((), ())), preferred_element_type=jnp.float32
        )
        grad_in = term if grad_in is None else grad_in + term
    grad_in = grad_in.astype(jnp.bfloat16)

    def span_of(total, first_span):
        return lax.dynamic_slice_in_dim(total, first_span * span, span, 0)

    summed_grads = tuple(span_of(total, (replica - 1) % replicas) for total in totals)
    for turn_index in range(1, replicas):
        summed_grads = shifted((summed_grads[0], summed_grads[1]), "ep", E)
        own = (replica - turn_index - 1) % replicas
        summed_grads = tuple(
            moved + span_of(total, own) for moved, total in zip(summed_grads, totals)
        )
    grad_scale = 1.0 / math.sqrt(2.0 * tokens_here * device_count / E)
    grad_w_in = (summed_grads[0] * grad_scale).T.astype(jnp.bfloat16)[None]
    grad_w_out = (summed_grads[1] * grad_scale).astype(jnp.bfloat16)[None]
    return (grad_in, grad_w_in, grad_w_out)

def solution(mesh):
    return jax.shard_map(
        shards,
        mesh=mesh,
        in_specs=(
            P("ep", None),
            P("ep", None),
            P("ep", None),
            P("ep", None),
            P("ep", None, "tp"),
            P("ep", "tp", None),
        ),
        out_specs=(P("ep", "tp"), P("ep", None, "tp"), P("ep", "tp", None)),
        check_vma=False,
    )
```

```python
import math

import jax
import jax.numpy as jnp
from jax import lax
from jax.sharding import PartitionSpec as P

E = 8


def shifted(value, axis, by):
    peers = lax.axis_size(axis)
    return lax.ppermute(value, axis, [(i, (i + by) % peers) for i in range(peers)])


def slot_positions(expert_ids, blocks, experts, capacity):
    flattened = expert_ids.reshape(blocks, -1)
    one_hot = (flattened[:, :, None] == jnp.arange(experts, dtype=jnp.int32)[None, None, :]).astype(
        jnp.int32
    )
    earlier = jnp.cumsum(one_hot, axis=1) - one_hot
    within = jnp.sum(one_hot * earlier, axis=2)
    block_ids = jnp.arange(blocks, dtype=jnp.int32)[:, None]
    return ((block_ids * experts + flattened) * capacity + within).reshape(-1)


def chip_then_link_sum(partial, j):
    quarter = partial.shape[0] // 4

    def rows(q):
        return lax.dynamic_slice_in_dim(partial, q * quarter, quarter, 0)

    keep = jnp.concatenate([rows(j), rows(j ^ 2)], axis=0)
    give = jnp.concatenate([rows(j ^ 1), rows(j ^ 3)], axis=0)
    keep = keep + lax.ppermute(give, "tp", [(i, i ^ 1) for i in range(4)])
    mine, send = keep[:quarter], keep[quarter:]
    return mine + lax.ppermute(send, "tp", [(i, i ^ 2) for i in range(4)])


def shards(features, cotangent, expert_ids, gate_levels, w_in, w_out):
    device_count = lax.axis_size("ep")
    replicas = device_count // E
    replica = lax.axis_index("ep") // E
    tokens_here = expert_ids.shape[0]
    sub_rows = tokens_here // replicas
    capacity = 3 * sub_rows // 8
    slot_count = device_count * capacity
    pair_count = 2 * tokens_here
    positions = slot_positions(expert_ids, replicas, E, capacity)
    slot_ids = jnp.arange(slot_count, dtype=jnp.int32)[:, None]
    choices = positions.reshape(tokens_here, 2)
    first_hit = choices[None, :, 0] == slot_ids
    second_hit = choices[None, :, 1] == slot_ids
    gates = gate_levels.astype(jnp.float32) / 16.0
    pick = (first_hit | second_hit).astype(jnp.bfloat16)
    pick_scaled = jnp.where(
        first_hit, gates[None, :, 0], jnp.where(second_hit, gates[None, :, 1], 0.0)
    ).astype(jnp.bfloat16)
    tp_size = lax.axis_size("tp")
    tp_index = lax.axis_index("tp")
    split = 4 if tp_size == 4 else (2 if tp_size % 2 == 0 else 1)

    part = tp_index % split

    def local_columns(table, selection):
        width = table.shape[1] // split
        mine = lax.dynamic_slice_in_dim(table, part * width, width, 1)
        return jnp.dot(selection, mine, preferred_element_type=jnp.float32).astype(jnp.bfloat16)

    def spread(mine, columns):
        width = columns // split
        pieces = [(mine, part)]
        if split == 4:
            across = lax.ppermute(mine, "tp", [(i, i ^ 2) for i in range(tp_size)])
            pieces.append((across, part ^ 2))
        if split >= 2:
            pieces += [
                (lax.ppermute(piece, "tp", [(i, i ^ 1) for i in range(tp_size)]), where ^ 1)
                for piece, where in pieces
            ]
        if split == 1:
            return mine
        whole = jnp.zeros((mine.shape[0], columns), jnp.bfloat16)
        for piece, where in pieces:
            whole = lax.dynamic_update_slice_in_dim(whole, piece, where * width, 1)
        return whole

    def over_ep(piece):
        return lax.all_to_all(piece, "ep", split_axis=0, concat_axis=0, tiled=True)

    moved_dy = over_ep(local_columns(cotangent, pick_scaled))
    local_x, moved_dy = lax.optimization_barrier((local_columns(features, pick), moved_dy))
    moved_x = over_ep(local_x)
    rows_dy = spread(moved_dy, cotangent.shape[1])
    rows_x = spread(moved_x, features.shape[1])
    piece_in = w_in[0]
    piece_out = w_out[0]
    span = piece_in.shape[1]
    weight_in = jnp.zeros((piece_in.shape[0], span * replicas), jnp.bfloat16)
    weight_out = jnp.zeros((span * replicas, piece_out.shape[1]), jnp.bfloat16)
    weight_in = lax.dynamic_update_slice_in_dim(weight_in, piece_in, replica * span, 1)
    weight_out = lax.dynamic_update_slice_in_dim(weight_out, piece_out, replica * span, 0)
    moving = (piece_in, piece_out)
    for turn_index in range(1, replicas):
        moving = shifted((moving[0], moving[1]), "ep", E)
        anchor = (replica - turn_index) % replicas
        weight_in = lax.dynamic_update_slice_in_dim(weight_in, moving[0], anchor * span, 1)
        weight_out = lax.dynamic_update_slice_in_dim(weight_out, moving[1], anchor * span, 0)
    pre = jnp.dot(rows_x, weight_in, preferred_element_type=jnp.float32)
    activated, gelu_back = jax.vjp(jax.nn.gelu, pre)
    act_rows = activated.astype(jnp.bfloat16)
    back_act = lax.dot_general(
        rows_dy, weight_out, (((1,), (1,)), ((), ())), preferred_element_type=jnp.float32
    )
    back_pre = gelu_back(back_act)[0].astype(jnp.bfloat16)
    partial = lax.dot_general(
        weight_in, back_pre, (((1,), (1,)), ((), ())), preferred_element_type=jnp.float32
    )
    if tp_size == 4:
        summed = chip_then_link_sum(partial, tp_index)
    else:
        summed = lax.psum_scatter(partial, "tp", scatter_dimension=0, tiled=True)
    def span_grads(first_span, span_total):
        width = span_total * span
        act_cols = lax.dynamic_slice_in_dim(act_rows, first_span * span, width, 1)
        pre_cols = lax.dynamic_slice_in_dim(back_pre, first_span * span, width, 1)
        grad_first = lax.dot_general(
            pre_cols, rows_x, (((0,), (0,)), ((), ())), preferred_element_type=jnp.float32
        )
        grad_second = lax.dot_general(
            act_cols, rows_dy, (((0,), (0,)), ((), ())), preferred_element_type=jnp.float32
        )
        return (grad_first, grad_second)

    summed_grads = span_grads((replica - 1) % replicas, 1)
    for turn_index in range(1, replicas):
        summed_grads = shifted((summed_grads[0], summed_grads[1]), "ep", E)
        own_grads = span_grads((replica - turn_index - 1) % replicas, 1)
        summed_grads = (summed_grads[0] + own_grads[0], summed_grads[1] + own_grads[1])
    grad_scale = 1.0 / math.sqrt(2.0 * tokens_here * device_count / E)
    grad_w_in = (summed_grads[0] * grad_scale).T.astype(jnp.bfloat16)[None]
    grad_w_out = (summed_grads[1] * grad_scale).astype(jnp.bfloat16)[None]
    leaving, grad_w_in, grad_w_out = lax.optimization_barrier(
        (summed.astype(jnp.bfloat16), grad_w_in, grad_w_out)
    )
    returned = lax.all_to_all(
        leaving, "ep", split_axis=1, concat_axis=1, tiled=True
    )
    grad_in = lax.dot_general(
        pick, returned, (((0,), (1,)), ((), ())), preferred_element_type=jnp.float32
    ).astype(jnp.bfloat16)
    return (grad_in, grad_w_in, grad_w_out)


def solution(mesh):
    return jax.shard_map(
        shards,
        mesh=mesh,
        in_specs=(
            P("ep", None),
            P("ep", None),
            P("ep", None),
            P("ep", None),
            P("ep", None, "tp"),
            P("ep", "tp", None),
        ),
        out_specs=(P("ep", "tp"), P("ep", None, "tp"), P("ep", "tp", None)),
        check_vma=False,
    )
```

```python
import math

import jax
import jax.numpy as jnp
from jax import lax
from jax.sharding import PartitionSpec as P

E = 8


def shifted(value, axis, by):
    peers = lax.axis_size(axis)
    return lax.ppermute(value, axis, [(i, (i + by) % peers) for i in range(peers)])


def slot_positions(expert_ids, blocks, experts, capacity):
    flattened = expert_ids.reshape(blocks, -1)
    one_hot = (flattened[:, :, None] == jnp.arange(experts, dtype=jnp.int32)[None, None, :]).astype(
        jnp.int32
    )
    earlier = jnp.cumsum(one_hot, axis=1) - one_hot
    within = jnp.sum(one_hot * earlier, axis=2)
    block_ids = jnp.arange(blocks, dtype=jnp.int32)[:, None]
    return ((block_ids * experts + flattened) * capacity + within).reshape(-1)


def exchange(value, axis, dimension):
    peers = lax.axis_size(axis)
    if peers > 8:
        return lax.all_to_all(value, axis, split_axis=dimension, concat_axis=dimension, tiled=True)
    me = lax.axis_index(axis)
    block = value.shape[dimension] // peers
    result = value
    for shift in range(1, peers):
        target = (me + shift) % peers
        source = (me + peers - shift) % peers
        outgoing = lax.dynamic_slice_in_dim(value, target * block, block, dimension)
        incoming = lax.ppermute(outgoing, axis, [(i, (i + shift) % peers) for i in range(peers)])
        result = lax.dynamic_update_slice_in_dim(result, incoming, source * block, dimension)
    return result


def chip_then_link_sum(partial, j):
    quarter = partial.shape[0] // 4

    def rows(q):
        return lax.dynamic_slice_in_dim(partial, q * quarter, quarter, 0)

    keep = jnp.concatenate([rows(j), rows(j ^ 2)], axis=0)
    give = jnp.concatenate([rows(j ^ 1), rows(j ^ 3)], axis=0)
    keep = keep + lax.ppermute(give, "tp", [(i, i ^ 1) for i in range(4)])
    mine, send = keep[:quarter], keep[quarter:]
    return mine + lax.ppermute(send, "tp", [(i, i ^ 2) for i in range(4)])


def shards(features, cotangent, expert_ids, gate_levels, w_in, w_out):
    device_count = lax.axis_size("ep")
    replicas = device_count // E
    replica = lax.axis_index("ep") // E
    tokens_here = expert_ids.shape[0]
    sub_rows = tokens_here // replicas
    capacity = 3 * sub_rows // 8
    slot_count = device_count * capacity
    pair_count = 2 * tokens_here
    positions = slot_positions(expert_ids, replicas, E, capacity)
    slot_ids = jnp.arange(slot_count, dtype=jnp.int32)[:, None]
    choices = positions.reshape(tokens_here, 2)
    first_hit = choices[None, :, 0] == slot_ids
    second_hit = choices[None, :, 1] == slot_ids
    gates = gate_levels.astype(jnp.float32) / 16.0
    pick = (first_hit | second_hit).astype(jnp.bfloat16)
    pick_scaled = jnp.where(
        first_hit, gates[None, :, 0], jnp.where(second_hit, gates[None, :, 1], 0.0)
    ).astype(jnp.bfloat16)
    tp_size = lax.axis_size("tp")
    tp_index = lax.axis_index("tp")
    split = 4 if tp_size == 4 else (2 if tp_size % 2 == 0 else 1)

    def dispatched(table, selection):
        width = table.shape[1] // split
        part = tp_index % split
        mine = lax.dynamic_slice_in_dim(table, part * width, width, 1)
        mine = jnp.dot(selection, mine, preferred_element_type=jnp.float32).astype(jnp.bfloat16)
        mine = exchange(mine, "ep", 0)
        pieces = [(mine, part)]
        if split == 4:
            across = lax.ppermute(mine, "tp", [(i, i ^ 2) for i in range(tp_size)])
            pieces.append((across, part ^ 2))
        if split >= 2:
            pieces += [
                (lax.ppermute(piece, "tp", [(i, i ^ 1) for i in range(tp_size)]), where ^ 1)
                for piece, where in pieces
            ]
        if split == 1:
            return mine
        whole = jnp.zeros((mine.shape[0], table.shape[1]), jnp.bfloat16)
        for piece, where in pieces:
            whole = lax.dynamic_update_slice_in_dim(whole, piece, where * width, 1)
        return whole

    rows_x = dispatched(features, pick)
    rows_dy = dispatched(cotangent, pick_scaled)
    piece_in = w_in[0]
    piece_out = w_out[0]
    span = piece_in.shape[1]
    weight_in = jnp.zeros((piece_in.shape[0], span * replicas), jnp.bfloat16)
    weight_out = jnp.zeros((span * replicas, piece_out.shape[1]), jnp.bfloat16)
    weight_in = lax.dynamic_update_slice_in_dim(weight_in, piece_in, replica * span, 1)
    weight_out = lax.dynamic_update_slice_in_dim(weight_out, piece_out, replica * span, 0)
    moving = (piece_in, piece_out)
    for turn_index in range(1, replicas):
        moving = shifted((moving[0], moving[1]), "ep", E)
        anchor = (replica - turn_index) % replicas
        weight_in = lax.dynamic_update_slice_in_dim(weight_in, moving[0], anchor * span, 1)
        weight_out = lax.dynamic_update_slice_in_dim(weight_out, moving[1], anchor * span, 0)
    pre = jnp.dot(rows_x, weight_in, preferred_element_type=jnp.float32)
    activated, gelu_back = jax.vjp(jax.nn.gelu, pre)
    act_rows = activated.astype(jnp.bfloat16)
    back_act = lax.dot_general(
        rows_dy, weight_out, (((1,), (1,)), ((), ())), preferred_element_type=jnp.float32
    )
    back_pre = gelu_back(back_act)[0].astype(jnp.bfloat16)
    partial = lax.dot_general(
        weight_in, back_pre, (((1,), (1,)), ((), ())), preferred_element_type=jnp.float32
    )
    if tp_size == 4:
        summed = chip_then_link_sum(partial, tp_index)
    else:
        summed = lax.psum_scatter(partial, "tp", scatter_dimension=0, tiled=True)
    def span_grads(first_span, span_total):
        width = span_total * span
        act_cols = lax.dynamic_slice_in_dim(act_rows, first_span * span, width, 1)
        pre_cols = lax.dynamic_slice_in_dim(back_pre, first_span * span, width, 1)
        grad_first = lax.dot_general(
            pre_cols, rows_x, (((0,), (0,)), ((), ())), preferred_element_type=jnp.float32
        )
        grad_second = lax.dot_general(
            act_cols, rows_dy, (((0,), (0,)), ((), ())), preferred_element_type=jnp.float32
        )
        return (grad_first, grad_second)

    summed_grads = span_grads((replica - 1) % replicas, 1)
    for turn_index in range(1, replicas):
        summed_grads = shifted((summed_grads[0], summed_grads[1]), "ep", E)
        own_grads = span_grads((replica - turn_index - 1) % replicas, 1)
        summed_grads = (summed_grads[0] + own_grads[0], summed_grads[1] + own_grads[1])
    grad_scale = 1.0 / math.sqrt(2.0 * tokens_here * device_count / E)
    grad_w_in = (summed_grads[0] * grad_scale).T.astype(jnp.bfloat16)[None]
    grad_w_out = (summed_grads[1] * grad_scale).astype(jnp.bfloat16)[None]
    leaving, grad_w_in, grad_w_out = lax.optimization_barrier(
        (summed.astype(jnp.bfloat16), grad_w_in, grad_w_out)
    )
    returned = exchange(leaving, "ep", 1)
    grad_in = lax.dot_general(
        pick, returned, (((0,), (1,)), ((), ())), preferred_element_type=jnp.float32
    ).astype(jnp.bfloat16)
    return (grad_in, grad_w_in, grad_w_out)


def solution(mesh):
    return jax.shard_map(
        shards,
        mesh=mesh,
        in_specs=(
            P("ep", None),
            P("ep", None),
            P("ep", None),
            P("ep", None),
            P("ep", None, "tp"),
            P("ep", "tp", None),
        ),
        out_specs=(P("ep", "tp"), P("ep", None, "tp"), P("ep", "tp", None)),
        check_vma=False,
    )
```

```python
import math

import jax
import jax.numpy as jnp
from jax import lax
from jax.sharding import PartitionSpec as P

E = 8


def shifted(value, axis, by):
    peers = lax.axis_size(axis)
    return lax.ppermute(value, axis, [(i, (i + by) % peers) for i in range(peers)])


def slot_positions(expert_ids, blocks, experts, capacity):
    flattened = expert_ids.reshape(blocks, -1)
    one_hot = (flattened[:, :, None] == jnp.arange(experts, dtype=jnp.int32)[None, None, :]).astype(
        jnp.int32
    )
    earlier = jnp.cumsum(one_hot, axis=1) - one_hot
    within = jnp.sum(one_hot * earlier, axis=2)
    block_ids = jnp.arange(blocks, dtype=jnp.int32)[:, None]
    return ((block_ids * experts + flattened) * capacity + within).reshape(-1)


def exchange(value, axis, dimension):
    peers = lax.axis_size(axis)
    if peers > 8:
        return lax.all_to_all(value, axis, split_axis=dimension, concat_axis=dimension, tiled=True)
    me = lax.axis_index(axis)
    block = value.shape[dimension] // peers
    result = value
    for shift in range(1, peers):
        target = (me + shift) % peers
        source = (me + peers - shift) % peers
        outgoing = lax.dynamic_slice_in_dim(value, target * block, block, dimension)
        incoming = lax.ppermute(outgoing, axis, [(i, (i + shift) % peers) for i in range(peers)])
        result = lax.dynamic_update_slice_in_dim(result, incoming, source * block, dimension)
    return result


def chip_then_link_sum(partial, j):
    quarter = partial.shape[0] // 4

    def rows(q):
        return lax.dynamic_slice_in_dim(partial, q * quarter, quarter, 0)

    keep = jnp.concatenate([rows(j), rows(j ^ 2)], axis=0)
    give = jnp.concatenate([rows(j ^ 1), rows(j ^ 3)], axis=0)
    keep = keep + lax.ppermute(give, "tp", [(i, i ^ 1) for i in range(4)])
    mine, send = keep[:quarter], keep[quarter:]
    return mine + lax.ppermute(send, "tp", [(i, i ^ 2) for i in range(4)])


def shards(features, cotangent, expert_ids, gate_levels, w_in, w_out):
    device_count = lax.axis_size("ep")
    replicas = device_count // E
    replica = lax.axis_index("ep") // E
    tokens_here = expert_ids.shape[0]
    sub_rows = tokens_here // replicas
    capacity = 3 * sub_rows // 8
    slot_count = device_count * capacity
    pair_count = 2 * tokens_here
    positions = slot_positions(expert_ids, replicas, E, capacity)
    slot_ids = jnp.arange(slot_count, dtype=jnp.int32)[:, None]
    choices = positions.reshape(tokens_here, 2)
    first_hit = choices[None, :, 0] == slot_ids
    second_hit = choices[None, :, 1] == slot_ids
    gates = gate_levels.astype(jnp.float32) / 16.0
    pick = (first_hit | second_hit).astype(jnp.bfloat16)
    pick_scaled = jnp.where(
        first_hit, gates[None, :, 0], jnp.where(second_hit, gates[None, :, 1], 0.0)
    ).astype(jnp.bfloat16)
    tp_size = lax.axis_size("tp")
    tp_index = lax.axis_index("tp")
    split = 4 if tp_size == 4 else (2 if tp_size % 2 == 0 else 1)

    part = tp_index % split
    tables = (features, cotangent)
    widths = [table.shape[1] // split for table in tables]
    mine = jnp.concatenate(
        [
            jnp.dot(
                selection,
                lax.dynamic_slice_in_dim(table, part * width, width, 1),
                preferred_element_type=jnp.float32,
            ).astype(jnp.bfloat16)
            for table, selection, width in zip(tables, (pick, pick_scaled), widths)
        ],
        axis=1,
    )
    mine = exchange(mine, "ep", 0)
    pieces = [(mine, part)]
    if split == 4:
        across = lax.ppermute(mine, "tp", [(i, i ^ 2) for i in range(tp_size)])
        pieces.append((across, part ^ 2))
    if split >= 2:
        pieces += [
            (lax.ppermute(piece, "tp", [(i, i ^ 1) for i in range(tp_size)]), where ^ 1)
            for piece, where in pieces
        ]
    wholes = [jnp.zeros((slot_count, table.shape[1]), jnp.bfloat16) for table in tables]
    for piece, where in pieces:
        start = 0
        for index, width in enumerate(widths):
            wholes[index] = lax.dynamic_update_slice_in_dim(
                wholes[index], piece[:, start:start + width], where * width, 1
            )
            start += width
    rows_x, rows_dy = wholes
    piece_in = w_in[0]
    piece_out = w_out[0]
    span = piece_in.shape[1]
    weight_in = jnp.zeros((piece_in.shape[0], span * replicas), jnp.bfloat16)
    weight_out = jnp.zeros((span * replicas, piece_out.shape[1]), jnp.bfloat16)
    weight_in = lax.dynamic_update_slice_in_dim(weight_in, piece_in, replica * span, 1)
    weight_out = lax.dynamic_update_slice_in_dim(weight_out, piece_out, replica * span, 0)
    moving = (piece_in, piece_out)
    for turn_index in range(1, replicas):
        moving = shifted((moving[0], moving[1]), "ep", E)
        anchor = (replica - turn_index) % replicas
        weight_in = lax.dynamic_update_slice_in_dim(weight_in, moving[0], anchor * span, 1)
        weight_out = lax.dynamic_update_slice_in_dim(weight_out, moving[1], anchor * span, 0)
    pre = jnp.dot(rows_x, weight_in, preferred_element_type=jnp.float32)
    activated, gelu_back = jax.vjp(jax.nn.gelu, pre)
    act_rows = activated.astype(jnp.bfloat16)
    back_act = lax.dot_general(
        rows_dy, weight_out, (((1,), (1,)), ((), ())), preferred_element_type=jnp.float32
    )
    back_pre = gelu_back(back_act)[0].astype(jnp.bfloat16)
    partial = lax.dot_general(
        weight_in, back_pre, (((1,), (1,)), ((), ())), preferred_element_type=jnp.float32
    )
    if tp_size == 4:
        summed = chip_then_link_sum(partial, tp_index)
    else:
        summed = lax.psum_scatter(partial, "tp", scatter_dimension=0, tiled=True)
    def span_grads(first_span, span_total):
        width = span_total * span
        act_cols = lax.dynamic_slice_in_dim(act_rows, first_span * span, width, 1)
        pre_cols = lax.dynamic_slice_in_dim(back_pre, first_span * span, width, 1)
        grad_first = lax.dot_general(
            pre_cols, rows_x, (((0,), (0,)), ((), ())), preferred_element_type=jnp.float32
        )
        grad_second = lax.dot_general(
            act_cols, rows_dy, (((0,), (0,)), ((), ())), preferred_element_type=jnp.float32
        )
        return (grad_first, grad_second)

    summed_grads = span_grads((replica - 1) % replicas, 1)
    for turn_index in range(1, replicas):
        summed_grads = shifted((summed_grads[0], summed_grads[1]), "ep", E)
        own_grads = span_grads((replica - turn_index - 1) % replicas, 1)
        summed_grads = (summed_grads[0] + own_grads[0], summed_grads[1] + own_grads[1])
    grad_scale = 1.0 / math.sqrt(2.0 * tokens_here * device_count / E)
    grad_w_in = (summed_grads[0] * grad_scale).T.astype(jnp.bfloat16)[None]
    grad_w_out = (summed_grads[1] * grad_scale).astype(jnp.bfloat16)[None]
    leaving, grad_w_in, grad_w_out = lax.optimization_barrier(
        (summed.astype(jnp.bfloat16), grad_w_in, grad_w_out)
    )
    returned = exchange(leaving, "ep", 1)
    grad_in = lax.dot_general(
        pick, returned, (((0,), (1,)), ((), ())), preferred_element_type=jnp.float32
    ).astype(jnp.bfloat16)
    return (grad_in, grad_w_in, grad_w_out)


def solution(mesh):
    return jax.shard_map(
        shards,
        mesh=mesh,
        in_specs=(
            P("ep", None),
            P("ep", None),
            P("ep", None),
            P("ep", None),
            P("ep", None, "tp"),
            P("ep", "tp", None),
        ),
        out_specs=(P("ep", "tp"), P("ep", None, "tp"), P("ep", "tp", None)),
        check_vma=False,
    )
```

```python
import math

import jax
import jax.numpy as jnp
from jax import lax
from jax.sharding import PartitionSpec as P

E = 8


def shifted(value, axis, by):
    peers = lax.axis_size(axis)
    return lax.ppermute(value, axis, [(i, (i + by) % peers) for i in range(peers)])


def slot_positions(expert_ids, blocks, experts, capacity):
    flattened = expert_ids.reshape(blocks, -1)
    one_hot = (flattened[:, :, None] == jnp.arange(experts, dtype=jnp.int32)[None, None, :]).astype(
        jnp.int32
    )
    earlier = jnp.cumsum(one_hot, axis=1) - one_hot
    within = jnp.sum(one_hot * earlier, axis=2)
    block_ids = jnp.arange(blocks, dtype=jnp.int32)[:, None]
    return ((block_ids * experts + flattened) * capacity + within).reshape(-1)


def exchange(value, axis, dimension):
    peers = lax.axis_size(axis)
    if peers > 8:
        return lax.all_to_all(value, axis, split_axis=dimension, concat_axis=dimension, tiled=True)
    me = lax.axis_index(axis)
    block = value.shape[dimension] // peers
    result = value
    for shift in range(1, peers):
        target = (me + shift) % peers
        source = (me + peers - shift) % peers
        outgoing = lax.dynamic_slice_in_dim(value, target * block, block, dimension)
        incoming = lax.ppermute(outgoing, axis, [(i, (i + shift) % peers) for i in range(peers)])
        result = lax.dynamic_update_slice_in_dim(result, incoming, source * block, dimension)
    return result


def chip_then_link_sum(partial, j):
    quarter = partial.shape[0] // 4

    def rows(q):
        return lax.dynamic_slice_in_dim(partial, q * quarter, quarter, 0)

    keep = jnp.concatenate([rows(j), rows(j ^ 2)], axis=0)
    give = jnp.concatenate([rows(j ^ 1), rows(j ^ 3)], axis=0)
    keep = keep + lax.ppermute(give, "tp", [(i, i ^ 1) for i in range(4)])
    mine, send = keep[:quarter], keep[quarter:]
    return mine + lax.ppermute(send, "tp", [(i, i ^ 2) for i in range(4)])


def shards(features, cotangent, expert_ids, gate_levels, w_in, w_out):
    device_count = lax.axis_size("ep")
    replicas = device_count // E
    replica = lax.axis_index("ep") // E
    tokens_here = expert_ids.shape[0]
    sub_rows = tokens_here // replicas
    capacity = 3 * sub_rows // 8
    slot_count = device_count * capacity
    pair_count = 2 * tokens_here
    positions = slot_positions(expert_ids, replicas, E, capacity)
    slot_ids = jnp.arange(slot_count, dtype=jnp.int32)[:, None]
    choices = positions.reshape(tokens_here, 2)
    first_hit = choices[None, :, 0] == slot_ids
    second_hit = choices[None, :, 1] == slot_ids
    gates = gate_levels.astype(jnp.float32) / 16.0
    pick = (first_hit | second_hit).astype(jnp.bfloat16)
    pick_scaled = jnp.where(
        first_hit, gates[None, :, 0], jnp.where(second_hit, gates[None, :, 1], 0.0)
    ).astype(jnp.bfloat16)
    tp_size = lax.axis_size("tp")
    tp_index = lax.axis_index("tp")
    split = 4 if tp_size == 4 else (2 if tp_size % 2 == 0 else 1)

    def dispatched(table, selection):
        width = table.shape[1] // split
        part = tp_index % split
        mine = lax.dynamic_slice_in_dim(table, part * width, width, 1)
        mine = jnp.dot(selection, mine, preferred_element_type=jnp.float32).astype(jnp.bfloat16)
        mine = exchange(mine, "ep", 0)
        pieces = [(mine, part)]
        if split == 4:
            across = lax.ppermute(mine, "tp", [(i, i ^ 2) for i in range(tp_size)])
            pieces.append((across, part ^ 2))
        if split >= 2:
            pieces += [
                (lax.ppermute(piece, "tp", [(i, i ^ 1) for i in range(tp_size)]), where ^ 1)
                for piece, where in pieces
            ]
        if split == 1:
            return mine
        whole = jnp.zeros((mine.shape[0], table.shape[1]), jnp.bfloat16)
        for piece, where in pieces:
            whole = lax.dynamic_update_slice_in_dim(whole, piece, where * width, 1)
        return whole

    rows_x = dispatched(features, pick)
    rows_dy = dispatched(cotangent, pick_scaled)
    piece_in = w_in[0]
    piece_out = w_out[0]
    span = piece_in.shape[1]
    weight_in = jnp.zeros((piece_in.shape[0], span * replicas), jnp.bfloat16)
    weight_out = jnp.zeros((span * replicas, piece_out.shape[1]), jnp.bfloat16)
    weight_in = lax.dynamic_update_slice_in_dim(weight_in, piece_in, replica * span, 1)
    weight_out = lax.dynamic_update_slice_in_dim(weight_out, piece_out, replica * span, 0)
    moving = (piece_in, piece_out)
    for turn_index in range(1, replicas):
        moving = shifted((moving[0], moving[1]), "ep", E)
        anchor = (replica - turn_index) % replicas
        weight_in = lax.dynamic_update_slice_in_dim(weight_in, moving[0], anchor * span, 1)
        weight_out = lax.dynamic_update_slice_in_dim(weight_out, moving[1], anchor * span, 0)
    pre = jnp.dot(rows_x, weight_in, preferred_element_type=jnp.float32)
    activated, gelu_back = jax.vjp(jax.nn.gelu, pre)
    act_rows = activated.astype(jnp.bfloat16)
    back_act = lax.dot_general(
        rows_dy, weight_out, (((1,), (1,)), ((), ())), preferred_element_type=jnp.float32
    )
    back_pre = gelu_back(back_act)[0].astype(jnp.bfloat16)
    partial = lax.dot_general(
        weight_in, back_pre, (((1,), (1,)), ((), ())), preferred_element_type=jnp.float32
    )
    if tp_size == 4:
        summed = chip_then_link_sum(partial, tp_index)
    else:
        summed = lax.psum_scatter(partial, "tp", scatter_dimension=0, tiled=True)
    def span_grads(first_span, span_total):
        width = span_total * span
        act_cols = lax.dynamic_slice_in_dim(act_rows, first_span * span, width, 1)
        pre_cols = lax.dynamic_slice_in_dim(back_pre, first_span * span, width, 1)
        grad_first = lax.dot_general(
            pre_cols, rows_x, (((0,), (0,)), ((), ())), preferred_element_type=jnp.float32
        )
        grad_second = lax.dot_general(
            act_cols, rows_dy, (((0,), (0,)), ((), ())), preferred_element_type=jnp.float32
        )
        return (grad_first, grad_second)

    summed_grads = span_grads((replica - 1) % replicas, 1)
    for turn_index in range(1, replicas):
        summed_grads = shifted((summed_grads[0], summed_grads[1]), "ep", E)
        own_grads = span_grads((replica - turn_index - 1) % replicas, 1)
        summed_grads = (summed_grads[0] + own_grads[0], summed_grads[1] + own_grads[1])
    grad_scale = 1.0 / math.sqrt(2.0 * tokens_here * device_count / E)
    grad_w_in = (summed_grads[0] * grad_scale).T.astype(jnp.bfloat16)[None]
    grad_w_out = (summed_grads[1] * grad_scale).astype(jnp.bfloat16)[None]
    leaving, grad_w_in, grad_w_out = lax.optimization_barrier(
        (summed.astype(jnp.bfloat16), grad_w_in, grad_w_out)
    )
    returned = lax.all_to_all(leaving, "ep", split_axis=1, concat_axis=1, tiled=True)
    grad_in = lax.dot_general(
        pick, returned, (((0,), (1,)), ((), ())), preferred_element_type=jnp.float32
    ).astype(jnp.bfloat16)
    return (grad_in, grad_w_in, grad_w_out)


def solution(mesh):
    return jax.shard_map(
        shards,
        mesh=mesh,
        in_specs=(
            P("ep", None),
            P("ep", None),
            P("ep", None),
            P("ep", None),
            P("ep", None, "tp"),
            P("ep", "tp", None),
        ),
        out_specs=(P("ep", "tp"), P("ep", None, "tp"), P("ep", "tp", None)),
        check_vma=False,
    )
```

```python
import math

import jax
import jax.numpy as jnp
from jax import lax
from jax.sharding import PartitionSpec as P

E = 8


def shifted(value, axis, by):
    peers = lax.axis_size(axis)
    return lax.ppermute(value, axis, [(i, (i + by) % peers) for i in range(peers)])


def slot_positions(expert_ids, blocks, experts, capacity):
    flattened = expert_ids.reshape(blocks, -1)
    one_hot = (flattened[:, :, None] == jnp.arange(experts, dtype=jnp.int32)[None, None, :]).astype(
        jnp.int32
    )
    earlier = jnp.cumsum(one_hot, axis=1) - one_hot
    within = jnp.sum(one_hot * earlier, axis=2)
    block_ids = jnp.arange(blocks, dtype=jnp.int32)[:, None]
    return ((block_ids * experts + flattened) * capacity + within).reshape(-1)


def exchange(value, axis, dimension):
    peers = lax.axis_size(axis)
    if peers > 8:
        return lax.all_to_all(value, axis, split_axis=dimension, concat_axis=dimension, tiled=True)
    me = lax.axis_index(axis)
    block = value.shape[dimension] // peers
    result = value
    for shift in range(1, peers):
        target = (me + shift) % peers
        source = (me + peers - shift) % peers
        outgoing = lax.dynamic_slice_in_dim(value, target * block, block, dimension)
        incoming = lax.ppermute(outgoing, axis, [(i, (i + shift) % peers) for i in range(peers)])
        result = lax.dynamic_update_slice_in_dim(result, incoming, source * block, dimension)
    return result


def chip_then_link_sum(partial, j):
    quarter = partial.shape[0] // 4

    def rows(q):
        return lax.dynamic_slice_in_dim(partial, q * quarter, quarter, 0)

    keep = jnp.concatenate([rows(j), rows(j ^ 2)], axis=0)
    give = jnp.concatenate([rows(j ^ 1), rows(j ^ 3)], axis=0)
    keep = keep + lax.ppermute(give, "tp", [(i, i ^ 1) for i in range(4)])
    mine, send = keep[:quarter], keep[quarter:]
    return mine + lax.ppermute(send, "tp", [(i, i ^ 2) for i in range(4)])


def shards(features, cotangent, expert_ids, gate_levels, w_in, w_out):
    device_count = lax.axis_size("ep")
    replicas = device_count // E
    replica = lax.axis_index("ep") // E
    tokens_here = expert_ids.shape[0]
    sub_rows = tokens_here // replicas
    capacity = 3 * sub_rows // 8
    slot_count = device_count * capacity
    pair_count = 2 * tokens_here
    positions = slot_positions(expert_ids, replicas, E, capacity)
    slot_ids = jnp.arange(slot_count, dtype=jnp.int32)[:, None]
    choices = positions.reshape(tokens_here, 2)
    first_hit = choices[None, :, 0] == slot_ids
    second_hit = choices[None, :, 1] == slot_ids
    gates = gate_levels.astype(jnp.float32) / 16.0
    pick = (first_hit | second_hit).astype(jnp.bfloat16)
    pick_scaled = jnp.where(
        first_hit, gates[None, :, 0], jnp.where(second_hit, gates[None, :, 1], 0.0)
    ).astype(jnp.bfloat16)
    tp_size = lax.axis_size("tp")
    tp_index = lax.axis_index("tp")
    split = 4 if tp_size == 4 else (2 if tp_size % 2 == 0 else 1)

    part = tp_index % split

    def local_columns(table, selection):
        width = table.shape[1] // split
        mine = lax.dynamic_slice_in_dim(table, part * width, width, 1)
        return jnp.dot(selection, mine, preferred_element_type=jnp.float32).astype(jnp.bfloat16)

    def spread(mine, columns):
        width = columns // split
        pieces = [(mine, part)]
        if split == 4:
            across = lax.ppermute(mine, "tp", [(i, i ^ 2) for i in range(tp_size)])
            pieces.append((across, part ^ 2))
        if split >= 2:
            pieces += [
                (lax.ppermute(piece, "tp", [(i, i ^ 1) for i in range(tp_size)]), where ^ 1)
                for piece, where in pieces
            ]
        if split == 1:
            return mine
        whole = jnp.zeros((mine.shape[0], columns), jnp.bfloat16)
        for piece, where in pieces:
            whole = lax.dynamic_update_slice_in_dim(whole, piece, where * width, 1)
        return whole

    local_x = local_columns(features, pick)
    local_dy = local_columns(cotangent, pick_scaled)
    moved = exchange(jnp.concatenate([local_x, local_dy], axis=1), "ep", 0)
    rows_x = spread(moved[:, :local_x.shape[1]], features.shape[1])
    rows_dy = spread(moved[:, local_x.shape[1]:], cotangent.shape[1])
    piece_in = w_in[0]
    piece_out = w_out[0]
    span = piece_in.shape[1]
    weight_in = jnp.zeros((piece_in.shape[0], span * replicas), jnp.bfloat16)
    weight_out = jnp.zeros((span * replicas, piece_out.shape[1]), jnp.bfloat16)
    weight_in = lax.dynamic_update_slice_in_dim(weight_in, piece_in, replica * span, 1)
    weight_out = lax.dynamic_update_slice_in_dim(weight_out, piece_out, replica * span, 0)
    moving = (piece_in, piece_out)
    for turn_index in range(1, replicas):
        moving = shifted((moving[0], moving[1]), "ep", E)
        anchor = (replica - turn_index) % replicas
        weight_in = lax.dynamic_update_slice_in_dim(weight_in, moving[0], anchor * span, 1)
        weight_out = lax.dynamic_update_slice_in_dim(weight_out, moving[1], anchor * span, 0)
    pre = jnp.dot(rows_x, weight_in, preferred_element_type=jnp.float32)
    activated, gelu_back = jax.vjp(jax.nn.gelu, pre)
    act_rows = activated.astype(jnp.bfloat16)
    back_act = lax.dot_general(
        rows_dy, weight_out, (((1,), (1,)), ((), ())), preferred_element_type=jnp.float32
    )
    back_pre = gelu_back(back_act)[0].astype(jnp.bfloat16)
    partial = lax.dot_general(
        weight_in, back_pre, (((1,), (1,)), ((), ())), preferred_element_type=jnp.float32
    )
    if tp_size == 4:
        summed = chip_then_link_sum(partial, tp_index)
    else:
        summed = lax.psum_scatter(partial, "tp", scatter_dimension=0, tiled=True)
    def span_grads(first_span, span_total):
        width = span_total * span
        act_cols = lax.dynamic_slice_in_dim(act_rows, first_span * span, width, 1)
        pre_cols = lax.dynamic_slice_in_dim(back_pre, first_span * span, width, 1)
        grad_first = lax.dot_general(
            pre_cols, rows_x, (((0,), (0,)), ((), ())), preferred_element_type=jnp.float32
        )
        grad_second = lax.dot_general(
            act_cols, rows_dy, (((0,), (0,)), ((), ())), preferred_element_type=jnp.float32
        )
        return (grad_first, grad_second)

    summed_grads = span_grads((replica - 1) % replicas, 1)
    for turn_index in range(1, replicas):
        summed_grads = shifted((summed_grads[0], summed_grads[1]), "ep", E)
        own_grads = span_grads((replica - turn_index - 1) % replicas, 1)
        summed_grads = (summed_grads[0] + own_grads[0], summed_grads[1] + own_grads[1])
    grad_scale = 1.0 / math.sqrt(2.0 * tokens_here * device_count / E)
    grad_w_in = (summed_grads[0] * grad_scale).T.astype(jnp.bfloat16)[None]
    grad_w_out = (summed_grads[1] * grad_scale).astype(jnp.bfloat16)[None]
    leaving, grad_w_in, grad_w_out = lax.optimization_barrier(
        (summed.astype(jnp.bfloat16), grad_w_in, grad_w_out)
    )
    returned = lax.all_to_all(leaving, "ep", split_axis=1, concat_axis=1, tiled=True)
    grad_in = lax.dot_general(
        pick, returned, (((0,), (1,)), ((), ())), preferred_element_type=jnp.float32
    ).astype(jnp.bfloat16)
    return (grad_in, grad_w_in, grad_w_out)


def solution(mesh):
    return jax.shard_map(
        shards,
        mesh=mesh,
        in_specs=(
            P("ep", None),
            P("ep", None),
            P("ep", None),
            P("ep", None),
            P("ep", None, "tp"),
            P("ep", "tp", None),
        ),
        out_specs=(P("ep", "tp"), P("ep", None, "tp"), P("ep", "tp", None)),
        check_vma=False,
    )
```

```python
import math

import jax
import jax.numpy as jnp
from jax import lax
from jax.sharding import PartitionSpec as P

E = 8


def shifted(value, axis, by):
    peers = lax.axis_size(axis)
    return lax.ppermute(value, axis, [(i, (i + by) % peers) for i in range(peers)])


def slot_positions(expert_ids, blocks, experts, capacity):
    flattened = expert_ids.reshape(blocks, -1)
    one_hot = (flattened[:, :, None] == jnp.arange(experts, dtype=jnp.int32)[None, None, :]).astype(
        jnp.int32
    )
    earlier = jnp.cumsum(one_hot, axis=1) - one_hot
    within = jnp.sum(one_hot * earlier, axis=2)
    block_ids = jnp.arange(blocks, dtype=jnp.int32)[:, None]
    return ((block_ids * experts + flattened) * capacity + within).reshape(-1)


def exchange(value, axis, dimension):
    peers = lax.axis_size(axis)
    if peers > 8:
        return lax.all_to_all(value, axis, split_axis=dimension, concat_axis=dimension, tiled=True)
    me = lax.axis_index(axis)
    block = value.shape[dimension] // peers
    result = value
    for shift in range(1, peers):
        target = (me + shift) % peers
        source = (me + peers - shift) % peers
        outgoing = lax.dynamic_slice_in_dim(value, target * block, block, dimension)
        incoming = lax.ppermute(outgoing, axis, [(i, (i + shift) % peers) for i in range(peers)])
        result = lax.dynamic_update_slice_in_dim(result, incoming, source * block, dimension)
    return result


def exchange_rotated(value, axis):
    peers = lax.axis_size(axis)
    me = lax.axis_index(axis)
    block = value.shape[0] // peers
    pieces = [lax.dynamic_slice_in_dim(value, me * block, block, 0)]
    for shift in range(1, peers):
        target = (me + peers - shift) % peers
        outgoing = lax.dynamic_slice_in_dim(value, target * block, block, 0)
        pairs = [(i, (i + peers - shift) % peers) for i in range(peers)]
        pieces.append(lax.ppermute(outgoing, axis, pairs))
    return jnp.concatenate(pieces, axis=0)


def chip_then_link_sum(partial, j):
    quarter = partial.shape[0] // 4

    def rows(q):
        return lax.dynamic_slice_in_dim(partial, q * quarter, quarter, 0)

    keep = jnp.concatenate([rows(j), rows(j ^ 2)], axis=0)
    give = jnp.concatenate([rows(j ^ 1), rows(j ^ 3)], axis=0)
    keep = keep + lax.ppermute(give, "tp", [(i, i ^ 1) for i in range(4)])
    mine, send = keep[:quarter], keep[quarter:]
    return mine + lax.ppermute(send, "tp", [(i, i ^ 2) for i in range(4)])


def shards(features, cotangent, expert_ids, gate_levels, w_in, w_out):
    device_count = lax.axis_size("ep")
    replicas = device_count // E
    replica = lax.axis_index("ep") // E
    tokens_here = expert_ids.shape[0]
    sub_rows = tokens_here // replicas
    capacity = 3 * sub_rows // 8
    slot_count = device_count * capacity
    pair_count = 2 * tokens_here
    positions = slot_positions(expert_ids, replicas, E, capacity)
    slot_ids = jnp.arange(slot_count, dtype=jnp.int32)[:, None]
    choices = positions.reshape(tokens_here, 2)
    first_hit = choices[None, :, 0] == slot_ids
    second_hit = choices[None, :, 1] == slot_ids
    gates = gate_levels.astype(jnp.float32) / 16.0
    pick = (first_hit | second_hit).astype(jnp.bfloat16)
    pick_scaled = jnp.where(
        first_hit, gates[None, :, 0], jnp.where(second_hit, gates[None, :, 1], 0.0)
    ).astype(jnp.bfloat16)
    tp_size = lax.axis_size("tp")
    tp_index = lax.axis_index("tp")
    split = 4 if tp_size == 4 else (2 if tp_size % 2 == 0 else 1)

    part = tp_index % split

    def local_columns(table, selection):
        width = table.shape[1] // split
        mine = lax.dynamic_slice_in_dim(table, part * width, width, 1)
        return jnp.dot(selection, mine, preferred_element_type=jnp.float32).astype(jnp.bfloat16)

    def spread(mine, columns):
        width = columns // split
        pieces = [(mine, part)]
        if split == 4:
            across = lax.ppermute(mine, "tp", [(i, i ^ 2) for i in range(tp_size)])
            pieces.append((across, part ^ 2))
        if split >= 2:
            pieces += [
                (lax.ppermute(piece, "tp", [(i, i ^ 1) for i in range(tp_size)]), where ^ 1)
                for piece, where in pieces
            ]
        if split == 1:
            return mine
        whole = jnp.zeros((mine.shape[0], columns), jnp.bfloat16)
        for piece, where in pieces:
            whole = lax.dynamic_update_slice_in_dim(whole, piece, where * width, 1)
        return whole

    local_x = local_columns(features, pick)
    local_dy = local_columns(cotangent, pick_scaled)
    rotated = device_count <= 8
    joined = jnp.concatenate([local_x, local_dy], axis=1)
    if rotated:
        moved = exchange_rotated(joined, "ep")
    else:
        moved = lax.all_to_all(joined, "ep", split_axis=0, concat_axis=0, tiled=True)
    rows_x = spread(moved[:, :local_x.shape[1]], features.shape[1])
    rows_dy = spread(moved[:, local_x.shape[1]:], cotangent.shape[1])
    piece_in = w_in[0]
    piece_out = w_out[0]
    span = piece_in.shape[1]
    weight_in = jnp.zeros((piece_in.shape[0], span * replicas), jnp.bfloat16)
    weight_out = jnp.zeros((span * replicas, piece_out.shape[1]), jnp.bfloat16)
    weight_in = lax.dynamic_update_slice_in_dim(weight_in, piece_in, replica * span, 1)
    weight_out = lax.dynamic_update_slice_in_dim(weight_out, piece_out, replica * span, 0)
    moving = (piece_in, piece_out)
    for turn_index in range(1, replicas):
        moving = shifted((moving[0], moving[1]), "ep", E)
        anchor = (replica - turn_index) % replicas
        weight_in = lax.dynamic_update_slice_in_dim(weight_in, moving[0], anchor * span, 1)
        weight_out = lax.dynamic_update_slice_in_dim(weight_out, moving[1], anchor * span, 0)
    pre = jnp.dot(rows_x, weight_in, preferred_element_type=jnp.float32)
    activated, gelu_back = jax.vjp(jax.nn.gelu, pre)
    act_rows = activated.astype(jnp.bfloat16)
    back_act = lax.dot_general(
        rows_dy, weight_out, (((1,), (1,)), ((), ())), preferred_element_type=jnp.float32
    )
    back_pre = gelu_back(back_act)[0].astype(jnp.bfloat16)
    partial = lax.dot_general(
        weight_in, back_pre, (((1,), (1,)), ((), ())), preferred_element_type=jnp.float32
    )
    if tp_size == 4:
        summed = chip_then_link_sum(partial, tp_index)
    else:
        summed = lax.psum_scatter(partial, "tp", scatter_dimension=0, tiled=True)
    def span_grads(first_span, span_total):
        width = span_total * span
        act_cols = lax.dynamic_slice_in_dim(act_rows, first_span * span, width, 1)
        pre_cols = lax.dynamic_slice_in_dim(back_pre, first_span * span, width, 1)
        grad_first = lax.dot_general(
            pre_cols, rows_x, (((0,), (0,)), ((), ())), preferred_element_type=jnp.float32
        )
        grad_second = lax.dot_general(
            act_cols, rows_dy, (((0,), (0,)), ((), ())), preferred_element_type=jnp.float32
        )
        return (grad_first, grad_second)

    summed_grads = span_grads((replica - 1) % replicas, 1)
    for turn_index in range(1, replicas):
        summed_grads = shifted((summed_grads[0], summed_grads[1]), "ep", E)
        own_grads = span_grads((replica - turn_index - 1) % replicas, 1)
        summed_grads = (summed_grads[0] + own_grads[0], summed_grads[1] + own_grads[1])
    grad_scale = 1.0 / math.sqrt(2.0 * tokens_here * device_count / E)
    grad_w_in = (summed_grads[0] * grad_scale).T.astype(jnp.bfloat16)[None]
    grad_w_out = (summed_grads[1] * grad_scale).astype(jnp.bfloat16)[None]
    leaving, grad_w_in, grad_w_out = lax.optimization_barrier(
        (summed.astype(jnp.bfloat16), grad_w_in, grad_w_out)
    )
    if rotated:
        blocks = leaving.reshape(leaving.shape[0], device_count, capacity)
        leaving = jnp.roll(blocks, lax.axis_index("ep"), axis=1).reshape(leaving.shape)
    returned = lax.all_to_all(leaving, "ep", split_axis=1, concat_axis=1, tiled=True)
    grad_in = lax.dot_general(
        pick, returned, (((0,), (1,)), ((), ())), preferred_element_type=jnp.float32
    ).astype(jnp.bfloat16)
    return (grad_in, grad_w_in, grad_w_out)


def solution(mesh):
    return jax.shard_map(
        shards,
        mesh=mesh,
        in_specs=(
            P("ep", None),
            P("ep", None),
            P("ep", None),
            P("ep", None),
            P("ep", None, "tp"),
            P("ep", "tp", None),
        ),
        out_specs=(P("ep", "tp"), P("ep", None, "tp"), P("ep", "tp", None)),
        check_vma=False,
    )
```

```python
import math

import jax
import jax.numpy as jnp
from jax import lax
from jax.sharding import PartitionSpec as P

E = 8


def shifted(value, axis, by):
    peers = lax.axis_size(axis)
    return lax.ppermute(value, axis, [(i, (i + by) % peers) for i in range(peers)])


def slot_positions(expert_ids, blocks, experts, capacity):
    flattened = expert_ids.reshape(blocks, -1)
    one_hot = (flattened[:, :, None] == jnp.arange(experts, dtype=jnp.int32)[None, None, :]).astype(
        jnp.int32
    )
    earlier = jnp.cumsum(one_hot, axis=1) - one_hot
    within = jnp.sum(one_hot * earlier, axis=2)
    block_ids = jnp.arange(blocks, dtype=jnp.int32)[:, None]
    return ((block_ids * experts + flattened) * capacity + within).reshape(-1)


def exchange(value, axis, dimension):
    peers = lax.axis_size(axis)
    if peers > 8:
        return lax.all_to_all(value, axis, split_axis=dimension, concat_axis=dimension, tiled=True)
    me = lax.axis_index(axis)
    block = value.shape[dimension] // peers
    result = value
    for shift in range(1, peers):
        target = (me + shift) % peers
        source = (me + peers - shift) % peers
        outgoing = lax.dynamic_slice_in_dim(value, target * block, block, dimension)
        incoming = lax.ppermute(outgoing, axis, [(i, (i + shift) % peers) for i in range(peers)])
        result = lax.dynamic_update_slice_in_dim(result, incoming, source * block, dimension)
    return result


def chip_then_link_sum(partial, j):
    quarter = partial.shape[0] // 4

    def rows(q):
        return lax.dynamic_slice_in_dim(partial, q * quarter, quarter, 0)

    keep = jnp.concatenate([rows(j), rows(j ^ 2)], axis=0)
    give = jnp.concatenate([rows(j ^ 1), rows(j ^ 3)], axis=0)
    keep = keep + lax.ppermute(give, "tp", [(i, i ^ 1) for i in range(4)])
    mine, send = keep[:quarter], keep[quarter:]
    return mine + lax.ppermute(send, "tp", [(i, i ^ 2) for i in range(4)])


def shards(features, cotangent, expert_ids, gate_levels, w_in, w_out):
    device_count = lax.axis_size("ep")
    replicas = device_count // E
    replica = lax.axis_index("ep") // E
    tokens_here = expert_ids.shape[0]
    sub_rows = tokens_here // replicas
    capacity = 3 * sub_rows // 8
    slot_count = device_count * capacity
    pair_count = 2 * tokens_here
    positions = slot_positions(expert_ids, replicas, E, capacity)
    slot_ids = jnp.arange(slot_count, dtype=jnp.int32)[:, None]
    choices = positions.reshape(tokens_here, 2)
    first_hit = choices[None, :, 0] == slot_ids
    second_hit = choices[None, :, 1] == slot_ids
    gates = gate_levels.astype(jnp.float32) / 16.0
    pick = (first_hit | second_hit).astype(jnp.bfloat16)
    pick_scaled = jnp.where(
        first_hit, gates[None, :, 0], jnp.where(second_hit, gates[None, :, 1], 0.0)
    ).astype(jnp.bfloat16)
    tp_size = lax.axis_size("tp")
    tp_index = lax.axis_index("tp")
    split = 4 if tp_size == 4 else (2 if tp_size % 2 == 0 else 1)

    part = tp_index % split

    def local_columns(table, selection):
        width = table.shape[1] // split
        mine = lax.dynamic_slice_in_dim(table, part * width, width, 1)
        return jnp.dot(selection, mine, preferred_element_type=jnp.float32).astype(jnp.bfloat16)

    def spread(mine, columns):
        width = columns // split
        pieces = [(mine, part)]
        if split == 4:
            across = lax.ppermute(mine, "tp", [(i, i ^ 2) for i in range(tp_size)])
            pieces.append((across, part ^ 2))
        if split >= 2:
            pieces += [
                (lax.ppermute(piece, "tp", [(i, i ^ 1) for i in range(tp_size)]), where ^ 1)
                for piece, where in pieces
            ]
        if split == 1:
            return mine
        whole = jnp.zeros((mine.shape[0], columns), jnp.bfloat16)
        for piece, where in pieces:
            whole = lax.dynamic_update_slice_in_dim(whole, piece, where * width, 1)
        return whole

    def over_ep(piece):
        return exchange(piece, "ep", 0)

    moved_dy = over_ep(local_columns(cotangent, pick_scaled))
    local_x, moved_dy = lax.optimization_barrier((local_columns(features, pick), moved_dy))
    moved_x = over_ep(local_x)
    rows_dy = spread(moved_dy, cotangent.shape[1])
    rows_x = spread(moved_x, features.shape[1])
    piece_in = w_in[0]
    piece_out = w_out[0]
    span = piece_in.shape[1]
    weight_in = jnp.zeros((piece_in.shape[0], span * replicas), jnp.bfloat16)
    weight_out = jnp.zeros((span * replicas, piece_out.shape[1]), jnp.bfloat16)
    weight_in = lax.dynamic_update_slice_in_dim(weight_in, piece_in, replica * span, 1)
    weight_out = lax.dynamic_update_slice_in_dim(weight_out, piece_out, replica * span, 0)
    moving = (piece_in, piece_out)
    for turn_index in range(1, replicas):
        moving = shifted((moving[0], moving[1]), "ep", E)
        anchor = (replica - turn_index) % replicas
        weight_in = lax.dynamic_update_slice_in_dim(weight_in, moving[0], anchor * span, 1)
        weight_out = lax.dynamic_update_slice_in_dim(weight_out, moving[1], anchor * span, 0)
    pre = jnp.dot(rows_x, weight_in, preferred_element_type=jnp.float32)
    activated, gelu_back = jax.vjp(jax.nn.gelu, pre)
    act_rows = activated.astype(jnp.bfloat16)
    back_act = lax.dot_general(
        rows_dy, weight_out, (((1,), (1,)), ((), ())), preferred_element_type=jnp.float32
    )
    back_pre = gelu_back(back_act)[0].astype(jnp.bfloat16)
    partial = lax.dot_general(
        weight_in, back_pre, (((1,), (1,)), ((), ())), preferred_element_type=jnp.float32
    )
    if tp_size == 4:
        summed = chip_then_link_sum(partial, tp_index)
    else:
        summed = lax.psum_scatter(partial, "tp", scatter_dimension=0, tiled=True)
    def span_grads(first_span, span_total):
        width = span_total * span
        act_cols = lax.dynamic_slice_in_dim(act_rows, first_span * span, width, 1)
        pre_cols = lax.dynamic_slice_in_dim(back_pre, first_span * span, width, 1)
        grad_first = lax.dot_general(
            pre_cols, rows_x, (((0,), (0,)), ((), ())), preferred_element_type=jnp.float32
        )
        grad_second = lax.dot_general(
            act_cols, rows_dy, (((0,), (0,)), ((), ())), preferred_element_type=jnp.float32
        )
        return (grad_first, grad_second)

    summed_grads = span_grads((replica - 1) % replicas, 1)
    for turn_index in range(1, replicas):
        summed_grads = shifted((summed_grads[0], summed_grads[1]), "ep", E)
        own_grads = span_grads((replica - turn_index - 1) % replicas, 1)
        summed_grads = (summed_grads[0] + own_grads[0], summed_grads[1] + own_grads[1])
    grad_scale = 1.0 / math.sqrt(2.0 * tokens_here * device_count / E)
    grad_w_in = (summed_grads[0] * grad_scale).T.astype(jnp.bfloat16)[None]
    grad_w_out = (summed_grads[1] * grad_scale).astype(jnp.bfloat16)[None]
    leaving, grad_w_in, grad_w_out = lax.optimization_barrier(
        (summed.astype(jnp.bfloat16), grad_w_in, grad_w_out)
    )
    returned = lax.all_to_all(leaving, "ep", split_axis=1, concat_axis=1, tiled=True)
    grad_in = lax.dot_general(
        pick, returned, (((0,), (1,)), ((), ())), preferred_element_type=jnp.float32
    ).astype(jnp.bfloat16)
    return (grad_in, grad_w_in, grad_w_out)


def solution(mesh):
    return jax.shard_map(
        shards,
        mesh=mesh,
        in_specs=(
            P("ep", None),
            P("ep", None),
            P("ep", None),
            P("ep", None),
            P("ep", None, "tp"),
            P("ep", "tp", None),
        ),
        out_specs=(P("ep", "tp"), P("ep", None, "tp"), P("ep", "tp", None)),
        check_vma=False,
    )
```
